768 devices in a mesh: enc: 12 (over z), grp: 64 (over y, x, core).
Axes of the slice: x: 4, y: 8, z: 12, core: 2. Of those that a mesh axis runs over, the one named last changes fastest.
Arguments:
- query_raw: bfloat16 [147456, 1024], P(('enc', 'grp')), may hold values from -6 to 6
- key_raw: bfloat16 [147456, 1024], P(('enc', 'grp')), may hold values from -6 to 6
- value_rows: bfloat16 [147456, 1024], P(('enc', 'grp')), may hold values from -6 to 6
- out_cotangent: bfloat16 [147456, 1024], P(('enc', 'grp')), may hold values from -6 to 6
- image_ids: int32 [147456], P(('enc', 'grp')), may hold values from 0 to 15, as said below
- owners: int32 [64, 12, 12], P('grp'), may hold values from -1 to 11, as said below
- gains: float32 [2, 1024], replicated, may hold values from 0.1 to 1.9
Outputs:
- query_grad: bfloat16 [98304, 1024], P(('enc', 'grp'))
- key_grad: bfloat16 [98304, 1024], P(('enc', 'grp'))
- value_grad: bfloat16 [98304, 1024], P(('enc', 'grp'))
- gain_grad: float32 [2, 1024], P(None, 'grp')
The draws below stay inside these ranges and needn't reach their ends.
Inputs may be any that keep to these rules, and one draw needn't show every extreme that they name: `image_ids`: inside each piece of 16 rows the number is 0 at the first row and rises by 0 or 1 from row to row. `owners`: A loader's live slots come first; a loader gives at most 1 pieces to one owner and some loader of each group gives exactly 1 to every owner; every owner receives exactly 8 pieces of its group.
All inputs are finite; a program needn't handle non-finite values.
Results may differ from the reference program's by a relative error of at most 0.0073.
Values may be sent and summed in bfloat16 or wider, within the bound.
No kernel may reach another device: no remote copies, remote signals or barrier semaphores. Data moves between devices by JAX's collectives and lax.ppermute only.
A program may use at most 32 MiB of HBM per device.

```python
import jax
import jax.numpy as jnp
from jax import lax

HEADS = 16
HD = 64
F = 1024
PIECE = 16
PMAX = 12
P_OWN = 8
ROWS = 147456
OUT_ROWS = 98304
N_ENC = 12
N_GRP = 64


def draw_owners(key, part):
    group_keys = jax.random.split(key, N_GRP)

    def one_group(group_key):
        first_key, second_key, third_key = jax.random.split(group_key, 3)
        pair_count = N_ENC // 2
        largest_shift = PMAX - P_OWN
        shifts = jax.random.randint(first_key, (pair_count,), 0, largest_shift + 1)
        forced = jax.random.randint(second_key, (), 0, pair_count)
        shifts = jnp.where(jnp.arange(pair_count) == forced, largest_shift, shifts)
        direction = jax.random.randint(third_key, (pair_count,), 0, 2) * 2 - 1
        counts = jnp.stack([P_OWN + direction * shifts, P_OWN - direction * shifts], 1).reshape(N_ENC)
        live_flags = (jnp.arange(PMAX)[None, :] < counts[:, None]).astype(jnp.int32)
        flat_live = live_flags.reshape(-1)
        running = jnp.cumsum(flat_live) - flat_live
        owner_ids = jnp.where(flat_live > 0, running % N_ENC, -1)
        return owner_ids.reshape(N_ENC, PMAX).astype(jnp.int32)
    return jax.vmap(one_group)(group_keys)


def draw_image_ids(key, part):
    new_image = (jax.random.randint(key, (ROWS // PIECE, PIECE), 0, 8) == 0).astype(jnp.int32)
    first_piece = jnp.arange(ROWS // PIECE)[:, None] % PMAX == 0
    new_image = jnp.where(first_piece, 1, new_image)
    new_image = new_image.at[:, 0].set(1)
    image_num = jnp.cumsum(new_image, 1) - 1
    return image_num.reshape(ROWS).astype(jnp.int32)


def block_levels(rng, dims, cuts, smallest, top_value):
    gain = 1.0
    for axis_at, shards_of in cuts:
        steps = jax.random.uniform(jax.random.fold_in(jax.random.fold_in(rng, 6), axis_at), (shards_of,), jnp.float32, smallest / len(cuts), top_value / len(cuts))
        gain = gain * jnp.repeat(jnp.exp(steps), dims[axis_at] // shards_of).reshape((-1,) + (1,) * (len(dims) - 1 - axis_at))
    return gain


def noise(stream_key, shape, spread, most, pieces=(), kind=jnp.bfloat16):
    level = block_levels(stream_key, shape, pieces, -0.22, 0.18) if pieces else 1.0
    entries = jax.random.normal(stream_key, shape, jnp.float32) * spread * level
    return jnp.minimum(jnp.maximum(entries, -most), most).astype(kind)


def setup_inputs(seed: int = 0) -> dict:
    seeds = jax.random.split(jax.random.key(seed), 8)
    query_raw = noise(seeds[0], (ROWS, F), 1.0, 6.0, ((0, 768),))
    key_raw = noise(seeds[1], (ROWS, F), 1.0, 6.0, ((0, 768),))
    value_rows = noise(seeds[2], (ROWS, F), 1.0, 6.0, ((0, 768),))
    out_cotangent = noise(seeds[3], (ROWS, F), 1.0, 6.0, ((0, 768),))
    image_ids = draw_image_ids(jax.random.fold_in(seeds[7], 71), 0)
    owners = draw_owners(jax.random.fold_in(seeds[7], 71), 0)
    gains = jnp.clip(1.0 + 0.18 * jax.random.normal(seeds[6], (2, F), jnp.float32), 0.1, 1.9)
    return {"query_raw": query_raw, "key_raw": key_raw, "value_rows": value_rows, "out_cotangent": out_cotangent, "image_ids": image_ids, "owners": owners, "gains": gains}


epsilon = 1e-05

def product(form, left, right):
    return jnp.einsum(form, left.astype(jnp.float32), right.astype(jnp.float32))

def normalize(blocks, gain_row):
    num_pieces = blocks.shape[0]
    values_four = blocks.astype(jnp.float32).reshape(num_pieces, PIECE, HEADS, HD)
    centred = values_four - lax.optimization_barrier(jnp.mean(values_four, -1, keepdims=True))
    inv_scale = lax.rsqrt(lax.optimization_barrier(jnp.mean(centred * centred, -1, keepdims=True)) + epsilon)
    normed = centred * inv_scale
    return (normed, inv_scale, (normed * gain_row).astype(jnp.bfloat16))

def norm_back(d_hat, normed, inv_scale, gain_row, live_flags):
    d_norm = d_hat * gain_row
    d_input = inv_scale * (d_norm - lax.optimization_barrier(jnp.mean(d_norm, -1, keepdims=True)) - normed * lax.optimization_barrier(jnp.mean(d_norm * normed, -1, keepdims=True)))
    gain_term = lax.optimization_barrier(jnp.sum(d_hat * normed * live_flags[:, None, None, None], (0, 1)))
    return (d_input, gain_term.reshape(-1))

def piece_grads(query_rows, key_rows, value_rows, cotangent, image_num, gains, live_flags):
    num_pieces = query_rows.shape[0]
    four_shape = (num_pieces, PIECE, HEADS, HD)
    gain_query = gains[0].reshape(HEADS, HD)
    gain_key = gains[1].reshape(HEADS, HD)
    q_norm, q_scale, q_hat = normalize(query_rows, gain_query)
    k_norm, k_scale, k_hat = normalize(key_rows, gain_key)
    values_four = value_rows.reshape(four_shape)
    cot_four = cotangent.reshape(four_shape)
    factor = HD ** (-0.5)
    scores = product('bihd,bjhd->bhij', q_hat, k_hat) * factor
    same_image = image_num[:, None, :, None] == image_num[:, None, None, :]
    weights = jnp.where(same_image, jnp.exp(scores), 0.0)
    probs = weights / lax.optimization_barrier(jnp.sum(weights, -1, keepdims=True))
    probs_b = probs.astype(jnp.bfloat16)
    attended = product('bhij,bjhd->bihd', probs_b, values_four)
    row_delta = lax.optimization_barrier(jnp.sum(cot_four.astype(jnp.float32) * attended, -1))
    d_value = product('bhij,bihd->bjhd', probs_b, cot_four).astype(jnp.bfloat16)
    d_prob = product('bihd,bjhd->bhij', cot_four, values_four)
    d_score = (probs * (d_prob - jnp.transpose(row_delta, (0, 2, 1))[..., None]) * factor).astype(jnp.bfloat16)
    d_qhat = product('bhij,bjhd->bihd', d_score, k_hat)
    d_khat = product('bhij,bihd->bjhd', d_score, q_hat)
    d_query, term_query = norm_back(d_qhat, q_norm, q_scale, gain_query, live_flags)
    d_key, term_key = norm_back(d_khat, k_norm, k_scale, gain_key, live_flags)
    flat_shape = (num_pieces, PIECE, HEADS * HD)
    return (d_query.reshape(flat_shape).astype(jnp.bfloat16), d_key.reshape(flat_shape).astype(jnp.bfloat16), d_value.reshape(flat_shape), jnp.stack([term_query, term_key]))

def reference(query_raw, key_raw, value_rows, out_cotangent, image_ids, owners, gains):
    dev_blocks = N_ENC * N_GRP
    feat = HEADS * HD
    owner_piece = jnp.transpose(owners, (1, 0, 2)).reshape(dev_blocks, PMAX)
    live_all = (owner_piece >= 0).astype(jnp.float32)

    def device_step(total, inputs):
        q_b, k_b, v_b, d_b, i_b, l_b = inputs
        d_q, d_k, d_v, terms = piece_grads(q_b, k_b, v_b, d_b, i_b, gains, l_b)
        return (total + terms, (d_q, d_k, d_v))
    shaped = (dev_blocks, PMAX, PIECE, feat)
    total, outs = lax.scan(device_step, jnp.zeros((2, feat), jnp.float32), (query_raw.reshape(shaped), key_raw.reshape(shaped), value_rows.reshape(shaped), out_cotangent.reshape(shaped), image_ids.reshape(dev_blocks, PMAX, PIECE), live_all))
    group_view = owners.reshape(N_GRP, N_ENC * PMAX)
    owner_hit = (group_view[..., None] == jnp.arange(N_ENC, dtype=jnp.int32)[None, None, :]).astype(jnp.int32)
    slot_rank = lax.optimization_barrier(jnp.sum((jnp.cumsum(owner_hit, 1) - owner_hit) * owner_hit, -1))
    group_index = jnp.arange(N_GRP, dtype=jnp.int32)[:, None]
    out_pieces = OUT_ROWS // PIECE
    target = jnp.where(group_view >= 0, (group_view * N_GRP + group_index) * P_OWN + slot_rank, out_pieces)
    target = jnp.transpose(target.reshape(N_GRP, N_ENC, PMAX), (1, 0, 2)).reshape(-1).astype(jnp.int32)
    results = []
    for grads in outs:
        placed = jnp.zeros((out_pieces, PIECE, feat), jnp.bfloat16)
        placed = placed.at[target].set(grads.reshape(-1, PIECE, feat), mode='drop')
        results.append(placed.reshape(OUT_ROWS, feat))
    gain_grad = total / jnp.sqrt(jnp.float32(OUT_ROWS))
    return (results[0], results[1], results[2], gain_grad)
```

```python
import math

import jax
import jax.numpy as jnp
from jax import lax
from jax.sharding import PartitionSpec as P

HEADS = 16
HD = 64
PIECE = 16
PMAX = 12
P_OWN = 8


epsilon = 1e-05


def normalize(blocks, gain_row):
    num_pieces = blocks.shape[0]
    values_four = blocks.astype(jnp.float32).reshape(num_pieces, PIECE, HEADS, HD)
    centred = values_four - jnp.mean(values_four, -1, keepdims=True)
    inv_scale = lax.rsqrt(jnp.mean(centred * centred, -1, keepdims=True) + epsilon)
    normed = centred * inv_scale
    return (normed, inv_scale, (normed * gain_row).astype(jnp.bfloat16))


def norm_back(d_hat, normed, inv_scale, gain_row, live_flags):
    d_norm = d_hat * gain_row
    d_input = inv_scale * (
        d_norm
        - jnp.mean(d_norm, -1, keepdims=True)
        - normed * jnp.mean(d_norm * normed, -1, keepdims=True)
    )
    gain_term = jnp.sum(d_hat * normed * live_flags[:, None, None, None], (0, 1))
    return (d_input, gain_term.reshape(-1))


def piece_grads(query_rows, key_rows, value_rows, cotangent, image_num, gains, live_flags):
    num_pieces = query_rows.shape[0]
    four_shape = (num_pieces, PIECE, HEADS, HD)
    gain_query = gains[0].reshape(HEADS, HD)
    gain_key = gains[1].reshape(HEADS, HD)
    q_norm, q_scale, q_hat = normalize(query_rows, gain_query)
    k_norm, k_scale, k_hat = normalize(key_rows, gain_key)
    values_four = value_rows.reshape(four_shape)
    cot_four = cotangent.reshape(four_shape)
    factor = HD ** (-0.5)
    scores = (
        jnp.einsum("bihd,bjhd->bhij", q_hat, k_hat, preferred_element_type=jnp.float32) * factor
    )
    same_image = image_num[:, None, :, None] == image_num[:, None, None, :]
    weights = jnp.where(same_image, jnp.exp(scores), 0.0)
    probs = weights / jnp.sum(weights, -1, keepdims=True)
    probs_b = probs.astype(jnp.bfloat16)
    attended = jnp.einsum(
        "bhij,bjhd->bihd", probs_b, values_four, preferred_element_type=jnp.float32
    )
    row_delta = jnp.sum(cot_four.astype(jnp.float32) * attended, -1)
    d_value = jnp.einsum(
        "bhij,bihd->bjhd", probs_b, cot_four, preferred_element_type=jnp.float32
    ).astype(jnp.bfloat16)
    d_prob = jnp.einsum(
        "bihd,bjhd->bhij", cot_four, values_four, preferred_element_type=jnp.float32
    )
    d_score = (probs * (d_prob - jnp.transpose(row_delta, (0, 2, 1))[..., None]) * factor).astype(
        jnp.bfloat16
    )
    d_qhat = jnp.einsum("bhij,bjhd->bihd", d_score, k_hat, preferred_element_type=jnp.float32)
    d_khat = jnp.einsum("bhij,bihd->bjhd", d_score, q_hat, preferred_element_type=jnp.float32)
    d_query, term_query = norm_back(d_qhat, q_norm, q_scale, gain_query, live_flags)
    d_key, term_key = norm_back(d_khat, k_norm, k_scale, gain_key, live_flags)
    flat_shape = (num_pieces, PIECE, HEADS * HD)
    return (
        d_query.reshape(flat_shape).astype(jnp.bfloat16),
        d_key.reshape(flat_shape).astype(jnp.bfloat16),
        d_value.reshape(flat_shape),
        jnp.stack([term_query, term_key]),
    )


def send_slots(own_plan, enc_count, per_slot):
    owner_hit = (own_plan[:, None] == jnp.arange(enc_count, dtype=jnp.int32)[None, :]).astype(
        jnp.int32
    )
    slot_rank = jnp.sum((jnp.cumsum(owner_hit, 0) - owner_hit) * owner_hit, 1)
    slot_target = jnp.where(own_plan >= 0, own_plan * per_slot + slot_rank, -1)
    slot_ids = jnp.arange(enc_count * per_slot, dtype=jnp.int32)
    matches = (slot_target[None, :] == slot_ids[:, None]).astype(jnp.int32)
    slot_source = jnp.sum(matches * jnp.arange(PMAX, dtype=jnp.int32)[None, :], 1)
    slot_filled = jnp.sum(matches, 1) > 0
    return (slot_source, slot_filled)


def receive_order(group_plan, enc_rank, enc_count, per_slot):
    arrived = jnp.sum((group_plan == enc_rank).astype(jnp.int32), 1)
    live_slots = (
        (jnp.arange(per_slot, dtype=jnp.int32)[None, :] < arrived[:, None])
        .reshape(-1)
        .astype(jnp.int32)
    )
    live_order = jnp.cumsum(live_slots) - 1
    wanted = jnp.arange(P_OWN, dtype=jnp.int32)
    matches = ((live_order[None, :] == wanted[:, None]) & (live_slots[None, :] > 0)).astype(
        jnp.int32
    )
    return jnp.sum(matches * jnp.arange(enc_count * per_slot, dtype=jnp.int32)[None, :], 1)


def to_slots(pieces, slot_source, slot_filled):
    taken = jnp.take(pieces, slot_source, axis=0)
    mask_shape = (slot_filled.shape[0],) + (1,) * (pieces.ndim - 1)
    taken = jnp.where(slot_filled.reshape(mask_shape), taken, jnp.zeros_like(taken))
    return taken


def from_slots(received, arrival_order):
    return jnp.take(received, arrival_order, axis=0, mode="clip")


def local(query_raw, key_raw, value_rows, out_cotangent, image_ids, owners, gains):
    enc_count = lax.axis_size("enc")
    grp_count = lax.axis_size("grp")
    enc_rank = lax.axis_index("enc")
    per_slot = PMAX // enc_count
    feat = HEADS * HD
    group_plan = owners[0]
    own_plan = lax.dynamic_index_in_dim(group_plan, enc_rank, 0, keepdims=False)
    slot_source, slot_filled = send_slots(own_plan, enc_count, per_slot)
    arrival_order = receive_order(group_plan, enc_rank, enc_count, per_slot)
    piece_shape = (PMAX, PIECE, feat)
    live_flags = (own_plan >= 0).astype(jnp.float32)
    d_query, d_key, d_value, gain_terms = piece_grads(
        query_raw.reshape(piece_shape),
        key_raw.reshape(piece_shape),
        value_rows.reshape(piece_shape),
        out_cotangent.reshape(piece_shape),
        image_ids.reshape(PMAX, PIECE),
        gains,
        live_flags,
    )
    grads = jnp.concatenate((d_query, d_key, d_value), axis=-1)
    packed = jnp.take(grads, slot_source, axis=0, mode="clip")
    received = lax.all_to_all(packed, "enc", split_axis=0, concat_axis=0, tiled=True)
    mine = from_slots(received, arrival_order)
    cols = feat // grp_count
    by_grp = jnp.transpose(gain_terms.reshape(2, grp_count, cols), (1, 0, 2))
    grp_sum = jnp.sum(
        lax.all_to_all(by_grp, "grp", split_axis=0, concat_axis=0, tiled=True), axis=0
    )
    by_enc = jnp.broadcast_to(grp_sum[None], (enc_count, 2, cols))
    shares = jnp.sum(
        lax.all_to_all(by_enc, "enc", split_axis=0, concat_axis=0, tiled=True), axis=0
    )
    total_live = enc_count * grp_count * P_OWN * PIECE
    gain_grad = shares / math.sqrt(total_live)
    own_rows = P_OWN * PIECE
    mine = mine.reshape(own_rows, 3 * feat)
    return (
        mine[:, :feat],
        mine[:, feat : 2 * feat],
        mine[:, 2 * feat :],
        gain_grad,
    )


def solution(mesh):
    return jax.shard_map(
        local,
        mesh=mesh,
        in_specs=(
            P(("enc", "grp"), None),
            P(("enc", "grp"), None),
            P(("enc", "grp"), None),
            P(("enc", "grp"), None),
            P(("enc", "grp")),
            P("grp", None, None),
            P(),
        ),
        out_specs=(
            P(("enc", "grp"), None),
            P(("enc", "grp"), None),
            P(("enc", "grp"), None),
            P(None, "grp"),
        ),
        check_vma=False,
    )
```

```python
import math

import jax
import jax.numpy as jnp
from jax import lax
from jax.sharding import PartitionSpec as P

HEADS = 16
HD = 64
PIECE = 16
PMAX = 12
P_OWN = 8


epsilon = 1e-05


def normalize(blocks, gain_row):
    num_pieces = blocks.shape[0]
    values_four = blocks.astype(jnp.float32).reshape(num_pieces, PIECE, HEADS, HD)
    centred = values_four - jnp.mean(values_four, -1, keepdims=True)
    inv_scale = lax.rsqrt(jnp.mean(centred * centred, -1, keepdims=True) + epsilon)
    normed = centred * inv_scale
    return (normed, inv_scale, (normed * gain_row).astype(jnp.bfloat16))


def norm_back(d_hat, normed, inv_scale, gain_row, live_flags):
    d_norm = d_hat * gain_row
    d_input = inv_scale * (
        d_norm
        - jnp.mean(d_norm, -1, keepdims=True)
        - normed * jnp.mean(d_norm * normed, -1, keepdims=True)
    )
    gain_term = jnp.sum(d_hat * normed * live_flags[:, None, None, None], (0, 1))
    return (d_input, gain_term.reshape(-1))


def piece_grads(query_rows, key_rows, value_rows, cotangent, image_num, gains, live_flags):
    num_pieces = query_rows.shape[0]
    four_shape = (num_pieces, PIECE, HEADS, HD)
    gain_query = gains[0].reshape(HEADS, HD)
    gain_key = gains[1].reshape(HEADS, HD)
    q_norm, q_scale, q_hat = normalize(query_rows, gain_query)
    k_norm, k_scale, k_hat = normalize(key_rows, gain_key)
    values_four = value_rows.reshape(four_shape)
    cot_four = cotangent.reshape(four_shape)
    factor = HD ** (-0.5)
    scores = (
        jnp.einsum("bihd,bjhd->bhij", q_hat, k_hat, preferred_element_type=jnp.float32) * factor
    )
    same_image = image_num[:, None, :, None] == image_num[:, None, None, :]
    weights = jnp.where(same_image, jnp.exp(scores), 0.0)
    probs = weights / jnp.sum(weights, -1, keepdims=True)
    probs_b = probs.astype(jnp.bfloat16)
    attended = jnp.einsum(
        "bhij,bjhd->bihd", probs_b, values_four, preferred_element_type=jnp.float32
    )
    row_delta = jnp.sum(cot_four.astype(jnp.float32) * attended, -1)
    d_value = jnp.einsum(
        "bhij,bihd->bjhd", probs_b, cot_four, preferred_element_type=jnp.float32
    ).astype(jnp.bfloat16)
    d_prob = jnp.einsum(
        "bihd,bjhd->bhij", cot_four, values_four, preferred_element_type=jnp.float32
    )
    d_score = (probs * (d_prob - jnp.transpose(row_delta, (0, 2, 1))[..., None]) * factor).astype(
        jnp.bfloat16
    )
    d_qhat = jnp.einsum("bhij,bjhd->bihd", d_score, k_hat, preferred_element_type=jnp.float32)
    d_khat = jnp.einsum("bhij,bihd->bjhd", d_score, q_hat, preferred_element_type=jnp.float32)
    d_query, term_query = norm_back(d_qhat, q_norm, q_scale, gain_query, live_flags)
    d_key, term_key = norm_back(d_khat, k_norm, k_scale, gain_key, live_flags)
    flat_shape = (num_pieces, PIECE, HEADS * HD)
    return (
        d_query.reshape(flat_shape).astype(jnp.bfloat16),
        d_key.reshape(flat_shape).astype(jnp.bfloat16),
        d_value.reshape(flat_shape),
        jnp.stack([term_query, term_key]),
    )


def send_slots(own_plan, enc_count, per_slot):
    owner_hit = (own_plan[:, None] == jnp.arange(enc_count, dtype=jnp.int32)[None, :]).astype(
        jnp.int32
    )
    slot_rank = jnp.sum((jnp.cumsum(owner_hit, 0) - owner_hit) * owner_hit, 1)
    slot_target = jnp.where(own_plan >= 0, own_plan * per_slot + slot_rank, -1)
    slot_ids = jnp.arange(enc_count * per_slot, dtype=jnp.int32)
    matches = (slot_target[None, :] == slot_ids[:, None]).astype(jnp.int32)
    slot_source = jnp.sum(matches * jnp.arange(PMAX, dtype=jnp.int32)[None, :], 1)
    slot_filled = jnp.sum(matches, 1) > 0
    return (slot_source, slot_filled)


def receive_order(group_plan, enc_rank, enc_count, per_slot):
    arrived = jnp.sum((group_plan == enc_rank).astype(jnp.int32), 1)
    live_slots = (
        (jnp.arange(per_slot, dtype=jnp.int32)[None, :] < arrived[:, None])
        .reshape(-1)
        .astype(jnp.int32)
    )
    live_order = jnp.cumsum(live_slots) - 1
    wanted = jnp.arange(P_OWN, dtype=jnp.int32)
    matches = ((live_order[None, :] == wanted[:, None]) & (live_slots[None, :] > 0)).astype(
        jnp.int32
    )
    return jnp.sum(matches * jnp.arange(enc_count * per_slot, dtype=jnp.int32)[None, :], 1)


def to_slots(pieces, slot_source, slot_filled):
    taken = jnp.take(pieces, slot_source, axis=0)
    mask_shape = (slot_filled.shape[0],) + (1,) * (pieces.ndim - 1)
    taken = jnp.where(slot_filled.reshape(mask_shape), taken, jnp.zeros_like(taken))
    return taken


def from_slots(received, arrival_order):
    return jnp.take(received, arrival_order, axis=0, mode="clip")


def local(query_raw, key_raw, value_rows, out_cotangent, image_ids, owners, gains):
    enc_count = lax.axis_size("enc")
    grp_count = lax.axis_size("grp")
    enc_rank = lax.axis_index("enc")
    per_slot = PMAX // enc_count
    feat = HEADS * HD
    group_plan = owners[0]
    own_plan = lax.dynamic_index_in_dim(group_plan, enc_rank, 0, keepdims=False)
    slot_source, slot_filled = send_slots(own_plan, enc_count, per_slot)
    arrival_order = receive_order(group_plan, enc_rank, enc_count, per_slot)
    piece_shape = (PMAX, PIECE, feat)
    live_flags = (own_plan >= 0).astype(jnp.float32)
    d_query, d_key, d_value, gain_terms = piece_grads(
        query_raw.reshape(piece_shape),
        key_raw.reshape(piece_shape),
        value_rows.reshape(piece_shape),
        out_cotangent.reshape(piece_shape),
        image_ids.reshape(PMAX, PIECE),
        gains,
        live_flags,
    )
    cols = feat // grp_count
    by_grp = jnp.transpose(gain_terms.reshape(2, grp_count, cols), (1, 0, 2))
    grp_sum = jnp.sum(
        lax.all_to_all(by_grp, "grp", split_axis=0, concat_axis=0, tiled=True), axis=0
    )
    grp_hi = grp_sum.astype(jnp.bfloat16)
    grp_lo = (grp_sum - grp_hi.astype(jnp.float32)).astype(jnp.bfloat16)
    extra = jnp.concatenate((grp_hi, grp_lo), axis=0)
    extra = jnp.pad(extra, ((0, PIECE - 4), (0, 128 - cols)))
    extra = jnp.broadcast_to(extra[None], (PMAX, PIECE, 128))
    grads = jnp.concatenate((d_query, d_key, d_value, extra), axis=-1)
    packed = jnp.take(grads, slot_source, axis=0, mode="clip")
    received = lax.all_to_all(packed, "enc", split_axis=0, concat_axis=0, tiled=True)
    mine = from_slots(received[:, :, : 3 * feat], arrival_order)
    parts = received[:, 0:4, 3 * feat : 3 * feat + cols].astype(jnp.float32)
    shares = jnp.sum(parts[:, 0:2] + parts[:, 2:4], axis=0)
    total_live = enc_count * grp_count * P_OWN * PIECE
    gain_grad = shares / math.sqrt(total_live)
    own_rows = P_OWN * PIECE
    mine = mine.reshape(own_rows, 3 * feat)
    return (
        mine[:, :feat],
        mine[:, feat : 2 * feat],
        mine[:, 2 * feat :],
        gain_grad,
    )


def solution(mesh):
    return jax.shard_map(
        local,
        mesh=mesh,
        in_specs=(
            P(("enc", "grp"), None),
            P(("enc", "grp"), None),
            P(("enc", "grp"), None),
            P(("enc", "grp"), None),
            P(("enc", "grp")),
            P("grp", None, None),
            P(),
        ),
        out_specs=(
            P(("enc", "grp"), None),
            P(("enc", "grp"), None),
            P(("enc", "grp"), None),
            P(None, "grp"),
        ),
        check_vma=False,
    )
```

```python
import math

import jax
import jax.numpy as jnp
from jax import lax
from jax.sharding import PartitionSpec as P

HEADS = 16
HD = 64
PIECE = 16
PMAX = 12
P_OWN = 8


epsilon = 1e-05


def normalize(blocks, gain_row):
    num_pieces = blocks.shape[0]
    values_four = blocks.astype(jnp.float32).reshape(num_pieces, PIECE, HEADS, HD)
    centred = values_four - jnp.mean(values_four, -1, keepdims=True)
    inv_scale = lax.rsqrt(jnp.mean(centred * centred, -1, keepdims=True) + epsilon)
    normed = centred * inv_scale
    return (normed, inv_scale, (normed * gain_row).astype(jnp.bfloat16))


def norm_back(d_hat, normed, inv_scale, gain_row, live_flags):
    d_norm = d_hat * gain_row
    d_input = inv_scale * (
        d_norm
        - jnp.mean(d_norm, -1, keepdims=True)
        - normed * jnp.mean(d_norm * normed, -1, keepdims=True)
    )
    gain_term = jnp.sum(d_hat * normed * live_flags[:, None, None, None], (0, 1))
    return (d_input, gain_term.reshape(-1))


def piece_grads(query_rows, key_rows, value_rows, cotangent, image_num, gains, live_flags):
    num_pieces = query_rows.shape[0]
    four_shape = (num_pieces, PIECE, HEADS, HD)
    gain_query = gains[0].reshape(HEADS, HD)
    gain_key = gains[1].reshape(HEADS, HD)
    q_norm, q_scale, q_hat = normalize(query_rows, gain_query)
    k_norm, k_scale, k_hat = normalize(key_rows, gain_key)
    values_four = value_rows.reshape(four_shape)
    cot_four = cotangent.reshape(four_shape)
    factor = HD ** (-0.5)
    scores = (
        jnp.einsum("bihd,bjhd->bhij", q_hat, k_hat, preferred_element_type=jnp.float32) * factor
    )
    same_image = image_num[:, None, :, None] == image_num[:, None, None, :]
    weights = jnp.where(same_image, jnp.exp(scores), 0.0)
    probs = weights / jnp.sum(weights, -1, keepdims=True)
    probs_b = probs.astype(jnp.bfloat16)
    attended = jnp.einsum(
        "bhij,bjhd->bihd", probs_b, values_four, preferred_element_type=jnp.float32
    )
    row_delta = jnp.sum(cot_four.astype(jnp.float32) * attended, -1)
    d_value = jnp.einsum(
        "bhij,bihd->bjhd", probs_b, cot_four, preferred_element_type=jnp.float32
    ).astype(jnp.bfloat16)
    d_prob = jnp.einsum(
        "bihd,bjhd->bhij", cot_four, values_four, preferred_element_type=jnp.float32
    )
    d_score = (probs * (d_prob - jnp.transpose(row_delta, (0, 2, 1))[..., None]) * factor).astype(
        jnp.bfloat16
    )
    d_qhat = jnp.einsum("bhij,bjhd->bihd", d_score, k_hat, preferred_element_type=jnp.float32)
    d_khat = jnp.einsum("bhij,bihd->bjhd", d_score, q_hat, preferred_element_type=jnp.float32)
    d_query, term_query = norm_back(d_qhat, q_norm, q_scale, gain_query, live_flags)
    d_key, term_key = norm_back(d_khat, k_norm, k_scale, gain_key, live_flags)
    flat_shape = (num_pieces, PIECE, HEADS * HD)
    return (
        d_query.reshape(flat_shape).astype(jnp.bfloat16),
        d_key.reshape(flat_shape).astype(jnp.bfloat16),
        d_value.reshape(flat_shape),
        jnp.stack([term_query, term_key]),
    )


def normalize_rows(rows, gain_row):
    values = rows.astype(jnp.float32).reshape(rows.shape[0], HEADS, HD)
    centred = values - jnp.mean(values, -1, keepdims=True)
    inv_scale = lax.rsqrt(jnp.mean(centred * centred, -1, keepdims=True) + epsilon)
    normed = centred * inv_scale
    return (normed, inv_scale, (normed * gain_row).astype(jnp.bfloat16))


def row_norm_back(d_hat, normed, inv_scale, gain_row, live_rows):
    d_norm = d_hat * gain_row
    d_input = inv_scale * (
        d_norm
        - jnp.mean(d_norm, -1, keepdims=True)
        - normed * jnp.mean(d_norm * normed, -1, keepdims=True)
    )
    gain_term = jnp.sum(d_hat * normed * live_rows[:, None, None], 0)
    return (d_input, gain_term.reshape(-1))


def block_grads(query_rows, key_rows, value_rows, cotangent, piece_of, image_num, gains, live_rows):
    rows = query_rows.shape[0]
    three = (rows, HEADS, HD)
    gain_query = gains[0].reshape(HEADS, HD)
    gain_key = gains[1].reshape(HEADS, HD)
    q_norm, q_scale, q_hat = normalize_rows(query_rows, gain_query)
    k_norm, k_scale, k_hat = normalize_rows(key_rows, gain_key)
    values = value_rows.reshape(three)
    cot = cotangent.reshape(three)
    factor = HD ** (-0.5)
    f32 = jnp.float32
    scores = jnp.einsum("ihd,jhd->hij", q_hat, k_hat, preferred_element_type=f32) * factor
    same = (piece_of[:, None] == piece_of[None, :]) & (image_num[:, None] == image_num[None, :])
    weights = jnp.where(same[None], jnp.exp(scores), 0.0)
    probs = weights / jnp.sum(weights, -1, keepdims=True)
    probs_b = probs.astype(jnp.bfloat16)
    attended = jnp.einsum("hij,jhd->ihd", probs_b, values, preferred_element_type=f32)
    row_delta = jnp.sum(cot.astype(f32) * attended, -1)
    d_value = jnp.einsum("hij,ihd->jhd", probs_b, cot, preferred_element_type=f32)
    d_prob = jnp.einsum("ihd,jhd->hij", cot, values, preferred_element_type=f32)
    d_score = (probs * (d_prob - jnp.transpose(row_delta)[..., None]) * factor).astype(
        jnp.bfloat16
    )
    d_qhat = jnp.einsum("hij,jhd->ihd", d_score, k_hat, preferred_element_type=f32)
    d_khat = jnp.einsum("hij,ihd->jhd", d_score, q_hat, preferred_element_type=f32)
    d_query, term_query = row_norm_back(d_qhat, q_norm, q_scale, gain_query, live_rows)
    d_key, term_key = row_norm_back(d_khat, k_norm, k_scale, gain_key, live_rows)
    flat = (rows, HEADS * HD)
    return (
        d_query.reshape(flat).astype(jnp.bfloat16),
        d_key.reshape(flat).astype(jnp.bfloat16),
        d_value.reshape(flat).astype(jnp.bfloat16),
        jnp.stack([term_query, term_key]),
    )


def send_slots(own_plan, enc_count, per_slot):
    owner_hit = (own_plan[:, None] == jnp.arange(enc_count, dtype=jnp.int32)[None, :]).astype(
        jnp.int32
    )
    slot_rank = jnp.sum((jnp.cumsum(owner_hit, 0) - owner_hit) * owner_hit, 1)
    slot_target = jnp.where(own_plan >= 0, own_plan * per_slot + slot_rank, -1)
    slot_ids = jnp.arange(enc_count * per_slot, dtype=jnp.int32)
    matches = (slot_target[None, :] == slot_ids[:, None]).astype(jnp.int32)
    slot_source = jnp.sum(matches * jnp.arange(PMAX, dtype=jnp.int32)[None, :], 1)
    slot_filled = jnp.sum(matches, 1) > 0
    return (slot_source, slot_filled)


def receive_order(group_plan, enc_rank, enc_count, per_slot):
    arrived = jnp.sum((group_plan == enc_rank).astype(jnp.int32), 1)
    live_slots = (
        (jnp.arange(per_slot, dtype=jnp.int32)[None, :] < arrived[:, None])
        .reshape(-1)
        .astype(jnp.int32)
    )
    live_order = jnp.cumsum(live_slots) - 1
    wanted = jnp.arange(P_OWN, dtype=jnp.int32)
    matches = ((live_order[None, :] == wanted[:, None]) & (live_slots[None, :] > 0)).astype(
        jnp.int32
    )
    return jnp.sum(matches * jnp.arange(enc_count * per_slot, dtype=jnp.int32)[None, :], 1)


def to_slots(pieces, slot_source, slot_filled):
    taken = jnp.take(pieces, slot_source, axis=0)
    mask_shape = (slot_filled.shape[0],) + (1,) * (pieces.ndim - 1)
    taken = jnp.where(slot_filled.reshape(mask_shape), taken, jnp.zeros_like(taken))
    return taken


def from_slots(received, arrival_order):
    return jnp.take(received, arrival_order, axis=0, mode="clip")


def local(query_raw, key_raw, value_rows, out_cotangent, image_ids, owners, gains):
    enc_count = lax.axis_size("enc")
    grp_count = lax.axis_size("grp")
    enc_rank = lax.axis_index("enc")
    per_slot = PMAX // enc_count
    feat = HEADS * HD
    group_plan = owners[0]
    own_plan = lax.dynamic_index_in_dim(group_plan, enc_rank, 0, keepdims=False)
    slot_source, slot_filled = send_slots(own_plan, enc_count, per_slot)
    arrival_order = receive_order(group_plan, enc_rank, enc_count, per_slot)
    piece_shape = (PMAX, PIECE, feat)
    live_flags = (own_plan >= 0).astype(jnp.float32)
    live_rows = jnp.repeat(live_flags, PIECE)
    piece_of = jnp.repeat(jnp.arange(PMAX, dtype=jnp.int32), PIECE)
    d_query, d_key, d_value, gain_terms = block_grads(
        query_raw, key_raw, value_rows, out_cotangent, piece_of, image_ids, gains, live_rows
    )
    d_query = d_query.reshape(piece_shape)
    d_key = d_key.reshape(piece_shape)
    d_value = d_value.reshape(piece_shape)
    cols = feat // grp_count
    by_grp = jnp.transpose(gain_terms.reshape(2, grp_count, cols), (1, 0, 2))
    grp_sum = jnp.sum(
        lax.all_to_all(by_grp, "grp", split_axis=0, concat_axis=0, tiled=True), axis=0
    )
    grp_top = lax.reduce_precision(grp_sum, exponent_bits=8, mantissa_bits=7)
    grp_hi = grp_top.astype(jnp.bfloat16)
    grp_lo = (grp_sum - grp_top).astype(jnp.bfloat16)
    extra = jnp.concatenate((grp_hi, grp_lo), axis=0)
    extra = jnp.pad(extra, ((0, PIECE - 4), (0, 128 - cols)))
    extra = jnp.broadcast_to(extra[None], (PMAX, PIECE, 128))
    grads = jnp.concatenate((d_query, d_key, d_value, extra), axis=-1)
    packed = jnp.take(grads, slot_source, axis=0, mode="clip")
    received = lax.all_to_all(packed, "enc", split_axis=0, concat_axis=0, tiled=True)
    mine = from_slots(received[:, :, : 3 * feat], arrival_order)
    parts = received[:, 0:4, 3 * feat : 3 * feat + cols].astype(jnp.float32)
    shares = jnp.sum(parts[:, 0:2] + parts[:, 2:4], axis=0)
    total_live = enc_count * grp_count * P_OWN * PIECE
    gain_grad = shares / math.sqrt(total_live)
    own_rows = P_OWN * PIECE
    mine = mine.reshape(own_rows, 3 * feat)
    return (
        mine[:, :feat],
        mine[:, feat : 2 * feat],
        mine[:, 2 * feat :],
        gain_grad,
    )


def solution(mesh):
    return jax.shard_map(
        local,
        mesh=mesh,
        in_specs=(
            P(("enc", "grp"), None),
            P(("enc", "grp"), None),
            P(("enc", "grp"), None),
            P(("enc", "grp"), None),
            P(("enc", "grp")),
            P("grp", None, None),
            P(),
        ),
        out_specs=(
            P(("enc", "grp"), None),
            P(("enc", "grp"), None),
            P(("enc", "grp"), None),
            P(None, "grp"),
        ),
        check_vma=False,
    )
```

```python
import math

import jax
import jax.numpy as jnp
from jax import lax
from jax.sharding import PartitionSpec as P


HEADS = 16
HD = 64
PIECE = 16
PMAX = 12
P_OWN = 8


epsilon = 1e-05


def normalize_rows(rows, gain_row):
    values = rows.astype(jnp.float32).reshape(rows.shape[0], rows.shape[1] // HD, HD)
    centred = values - jnp.mean(values, -1, keepdims=True)
    inv_scale = lax.rsqrt(jnp.mean(centred * centred, -1, keepdims=True) + epsilon)
    normed = centred * inv_scale
    return (normed, inv_scale, (normed * gain_row).astype(jnp.bfloat16))


def row_norm_back(d_hat, normed, inv_scale, gain_row, live_rows):
    d_norm = d_hat * gain_row
    d_input = inv_scale * (
        d_norm
        - jnp.mean(d_norm, -1, keepdims=True)
        - normed * jnp.mean(d_norm * normed, -1, keepdims=True)
    )
    gain_term = jnp.sum(d_hat * normed * live_rows[:, None, None], 0)
    return (d_input, gain_term.reshape(-1))


def block_grads(query_rows, key_rows, value_rows, cotangent, piece_of, image_num, gains, live_rows):
    rows = query_rows.shape[0]
    heads = query_rows.shape[1] // HD
    three = (rows, heads, HD)
    gain_query = gains[0].reshape(heads, HD)
    gain_key = gains[1].reshape(heads, HD)
    q_norm, q_scale, q_hat = normalize_rows(query_rows, gain_query)
    k_norm, k_scale, k_hat = normalize_rows(key_rows, gain_key)
    values = value_rows.reshape(three)
    cot = cotangent.reshape(three)
    factor = HD ** (-0.5)
    f32 = jnp.float32
    scores = jnp.einsum("ihd,jhd->hij", q_hat, k_hat, preferred_element_type=f32) * factor
    same = (piece_of[:, None] == piece_of[None, :]) & (image_num[:, None] == image_num[None, :])
    weights = jnp.where(same[None], jnp.exp(scores), 0.0)
    probs = weights / jnp.sum(weights, -1, keepdims=True)
    probs_b = probs.astype(jnp.bfloat16)
    attended = jnp.einsum("hij,jhd->ihd", probs_b, values, preferred_element_type=f32)
    row_delta = jnp.sum(cot.astype(f32) * attended, -1)
    d_value = jnp.einsum("hij,ihd->jhd", probs_b, cot, preferred_element_type=f32)
    d_prob = jnp.einsum("ihd,jhd->hij", cot, values, preferred_element_type=f32)
    d_score = (probs * (d_prob - jnp.transpose(row_delta)[..., None]) * factor).astype(
        jnp.bfloat16
    )
    d_qhat = jnp.einsum("hij,jhd->ihd", d_score, k_hat, preferred_element_type=f32)
    d_khat = jnp.einsum("hij,ihd->jhd", d_score, q_hat, preferred_element_type=f32)
    d_query, term_query = row_norm_back(d_qhat, q_norm, q_scale, gain_query, live_rows)
    d_key, term_key = row_norm_back(d_khat, k_norm, k_scale, gain_key, live_rows)
    flat = (rows, heads * HD)
    return (
        d_query.reshape(flat).astype(jnp.bfloat16),
        d_key.reshape(flat).astype(jnp.bfloat16),
        d_value.reshape(flat).astype(jnp.bfloat16),
        jnp.stack([term_query, term_key]),
    )


def send_slots(own_plan, enc_count, per_slot):
    owner_hit = (own_plan[:, None] == jnp.arange(enc_count, dtype=jnp.int32)[None, :]).astype(
        jnp.int32
    )
    slot_rank = jnp.sum((jnp.cumsum(owner_hit, 0) - owner_hit) * owner_hit, 1)
    slot_target = jnp.where(own_plan >= 0, own_plan * per_slot + slot_rank, -1)
    slot_ids = jnp.arange(enc_count * per_slot, dtype=jnp.int32)
    matches = (slot_target[None, :] == slot_ids[:, None]).astype(jnp.int32)
    slot_source = jnp.sum(matches * jnp.arange(PMAX, dtype=jnp.int32)[None, :], 1)
    slot_filled = jnp.sum(matches, 1) > 0
    return (slot_source, slot_filled)


def receive_order(group_plan, enc_rank, enc_count, per_slot):
    arrived = jnp.sum((group_plan == enc_rank).astype(jnp.int32), 1)
    live_slots = (
        (jnp.arange(per_slot, dtype=jnp.int32)[None, :] < arrived[:, None])
        .reshape(-1)
        .astype(jnp.int32)
    )
    live_order = jnp.cumsum(live_slots) - 1
    wanted = jnp.arange(P_OWN, dtype=jnp.int32)
    matches = ((live_order[None, :] == wanted[:, None]) & (live_slots[None, :] > 0)).astype(
        jnp.int32
    )
    return jnp.sum(matches * jnp.arange(enc_count * per_slot, dtype=jnp.int32)[None, :], 1)


def from_slots(received, arrival_order):
    return jnp.take(received, arrival_order, axis=0, mode="clip")


def local_body(query_raw, key_raw, value_rows, out_cotangent, image_ids, owners, gains):
    enc_count = lax.axis_size("enc")
    grp_count = lax.axis_size("grp")
    enc_rank = lax.axis_index("enc")
    per_slot = PMAX // enc_count
    feat = HEADS * HD
    group_plan = owners[0]
    own_plan = lax.dynamic_index_in_dim(group_plan, enc_rank, 0, keepdims=False)
    slot_source, _ = send_slots(own_plan, enc_count, per_slot)
    arrival_order = receive_order(group_plan, enc_rank, enc_count, per_slot)
    live_flags = (own_plan >= 0).astype(jnp.float32)
    live_rows = jnp.repeat(live_flags, PIECE)
    piece_of = jnp.repeat(jnp.arange(PMAX, dtype=jnp.int32), PIECE)
    half = feat // 2
    halves = []
    terms = []
    for part in range(2):
        cut = slice(part * half, (part + 1) * half)
        d_query, d_key, d_value, part_terms = block_grads(
            query_raw[:, cut],
            key_raw[:, cut],
            value_rows[:, cut],
            out_cotangent[:, cut],
            piece_of,
            image_ids,
            gains[:, cut],
            live_rows,
        )
        grads = jnp.concatenate((d_query, d_key, d_value), axis=-1)
        grads = grads.reshape(PMAX, PIECE, 3 * half)
        terms.append(part_terms)
        if part == 1:
            gain_terms = jnp.concatenate(terms, axis=1)
            cols = feat // grp_count
            by_grp = jnp.transpose(gain_terms.reshape(2, grp_count, cols), (1, 0, 2))
            by_grp = lax.all_to_all(by_grp, "grp", split_axis=0, concat_axis=0, tiled=True)
            grp_sum = jnp.sum(by_grp, axis=0)
            grp_top = lax.reduce_precision(grp_sum, exponent_bits=8, mantissa_bits=7)
            grp_hi = grp_top.astype(jnp.bfloat16)
            grp_lo = (grp_sum - grp_top).astype(jnp.bfloat16)
            extra = jnp.concatenate((grp_hi, grp_lo), axis=0)
            extra = jnp.pad(extra, ((0, PIECE - 4), (0, 128 - cols)))
            extra = jnp.broadcast_to(extra[None], (PMAX, PIECE, 128))
            grads = jnp.concatenate((grads, extra), axis=-1)
        packed = jnp.take(grads, slot_source, axis=0, mode="clip")
        if part == 0:
            packed, query_raw, key_raw, value_rows, out_cotangent = lax.optimization_barrier(
                (packed, query_raw, key_raw, value_rows, out_cotangent)
            )
        received = lax.all_to_all(packed, "enc", split_axis=0, concat_axis=0, tiled=True)
        halves.append(from_slots(received[:, :, : 3 * half], arrival_order))
    parts = received[:, 0:4, 3 * half : 3 * half + cols].astype(jnp.float32)
    shares = jnp.sum(parts[:, 0:2] + parts[:, 2:4], axis=0)
    total_live = enc_count * grp_count * P_OWN * PIECE
    gain_grad = shares / math.sqrt(total_live)
    own_rows = P_OWN * PIECE
    outs = []
    for which in range(3):
        outs.append(
            jnp.concatenate(
                [h[:, :, which * half : (which + 1) * half] for h in halves], axis=-1
            ).reshape(own_rows, feat)
        )
    return (outs[0], outs[1], outs[2], gain_grad)


def solution(mesh):
    return jax.shard_map(
        local_body,
        mesh=mesh,
        in_specs=(
            P(("enc", "grp"), None),
            P(("enc", "grp"), None),
            P(("enc", "grp"), None),
            P(("enc", "grp"), None),
            P(("enc", "grp")),
            P("grp", None, None),
            P(),
        ),
        out_specs=(
            P(("enc", "grp"), None),
            P(("enc", "grp"), None),
            P(("enc", "grp"), None),
            P(None, "grp"),
        ),
        check_vma=False,
    )
```

```python
import math

import jax
import jax.numpy as jnp
from jax import lax
from jax.sharding import PartitionSpec as P


HEADS = 16
HD = 64
PIECE = 16
PMAX = 12
P_OWN = 8


epsilon = 1e-05


def normalize_rows(rows, gain_row):
    values = rows.astype(jnp.float32).reshape(rows.shape[0], HEADS, HD)
    centred = values - jnp.mean(values, -1, keepdims=True)
    inv_scale = lax.rsqrt(jnp.mean(centred * centred, -1, keepdims=True) + epsilon)
    normed = centred * inv_scale
    return (normed, inv_scale, (normed * gain_row).astype(jnp.bfloat16))


def row_norm_back(d_hat, normed, inv_scale, gain_row, live_rows):
    d_norm = d_hat * gain_row
    d_input = inv_scale * (
        d_norm
        - jnp.mean(d_norm, -1, keepdims=True)
        - normed * jnp.mean(d_norm * normed, -1, keepdims=True)
    )
    gain_term = jnp.sum(d_hat * normed * live_rows[:, None, None], 0)
    return (d_input, gain_term.reshape(-1))


def block_grads(query_rows, key_rows, value_rows, cotangent, piece_of, image_num, gains, live_rows):
    rows = query_rows.shape[0]
    three = (rows, HEADS, HD)
    gain_query = gains[0].reshape(HEADS, HD)
    gain_key = gains[1].reshape(HEADS, HD)
    q_norm, q_scale, q_hat = normalize_rows(query_rows, gain_query)
    k_norm, k_scale, k_hat = normalize_rows(key_rows, gain_key)
    values = value_rows.reshape(three)
    cot = cotangent.reshape(three)
    factor = HD ** (-0.5)
    f32 = jnp.float32
    scores = jnp.einsum("ihd,jhd->hij", q_hat, k_hat, preferred_element_type=f32) * factor
    same = (piece_of[:, None] == piece_of[None, :]) & (image_num[:, None] == image_num[None, :])
    weights = jnp.where(same[None], jnp.exp(scores), 0.0)
    probs = weights / jnp.sum(weights, -1, keepdims=True)
    probs_b = probs.astype(jnp.bfloat16)
    attended = jnp.einsum("hij,jhd->ihd", probs_b, values, preferred_element_type=f32)
    row_delta = jnp.sum(cot.astype(f32) * attended, -1)
    d_value = jnp.einsum("hij,ihd->jhd", probs_b, cot, preferred_element_type=f32)
    d_prob = jnp.einsum("ihd,jhd->hij", cot, values, preferred_element_type=f32)
    d_score = (probs * (d_prob - jnp.transpose(row_delta)[..., None]) * factor).astype(
        jnp.bfloat16
    )
    d_qhat = jnp.einsum("hij,jhd->ihd", d_score, k_hat, preferred_element_type=f32)
    d_khat = jnp.einsum("hij,ihd->jhd", d_score, q_hat, preferred_element_type=f32)
    d_query, term_query = row_norm_back(d_qhat, q_norm, q_scale, gain_query, live_rows)
    d_key, term_key = row_norm_back(d_khat, k_norm, k_scale, gain_key, live_rows)
    flat = (rows, HEADS * HD)
    return (
        d_query.reshape(flat).astype(jnp.bfloat16),
        d_key.reshape(flat).astype(jnp.bfloat16),
        d_value.reshape(flat).astype(jnp.bfloat16),
        jnp.stack([term_query, term_key]),
    )


def reduce_gain_terms(gain_terms, enc_count, grp_count):
    grp_rank = lax.axis_index("grp")
    current = gain_terms
    bit = grp_count // 2
    while bit >= 1:
        width = current.shape[1] // 2
        upper = (grp_rank // bit) % 2 == 1
        low_part = current[:, :width]
        high_part = current[:, width:]
        send = jnp.where(upper, low_part, high_part)
        keep = jnp.where(upper, high_part, low_part)
        pairs = [(i, i ^ bit) for i in range(grp_count)]
        current = keep + lax.ppermute(send, "grp", pairs)
        bit //= 2
    enc_rank = lax.axis_index("enc")
    gathered = [current]
    for shift in range(1, enc_count):
        pairs = [(i, (i + shift) % enc_count) for i in range(enc_count)]
        gathered.append(lax.ppermute(current, "enc", pairs))
    stacked = jnp.stack(gathered)
    source_order = (enc_rank - jnp.arange(enc_count, dtype=jnp.int32)) % enc_count
    return jnp.sum(jnp.take(stacked, source_order, axis=0, mode="clip"), axis=0)


def send_slots(own_plan, enc_count, per_slot):
    owner_hit = (own_plan[:, None] == jnp.arange(enc_count, dtype=jnp.int32)[None, :]).astype(
        jnp.int32
    )
    slot_rank = jnp.sum((jnp.cumsum(owner_hit, 0) - owner_hit) * owner_hit, 1)
    slot_target = jnp.where(own_plan >= 0, own_plan * per_slot + slot_rank, -1)
    slot_ids = jnp.arange(enc_count * per_slot, dtype=jnp.int32)
    matches = (slot_target[None, :] == slot_ids[:, None]).astype(jnp.int32)
    slot_source = jnp.sum(matches * jnp.arange(PMAX, dtype=jnp.int32)[None, :], 1)
    slot_filled = jnp.sum(matches, 1) > 0
    return (slot_source, slot_filled)


def receive_order(group_plan, enc_rank, enc_count, per_slot):
    arrived = jnp.sum((group_plan == enc_rank).astype(jnp.int32), 1)
    live_slots = (
        (jnp.arange(per_slot, dtype=jnp.int32)[None, :] < arrived[:, None])
        .reshape(-1)
        .astype(jnp.int32)
    )
    live_order = jnp.cumsum(live_slots) - 1
    wanted = jnp.arange(P_OWN, dtype=jnp.int32)
    matches = ((live_order[None, :] == wanted[:, None]) & (live_slots[None, :] > 0)).astype(
        jnp.int32
    )
    return jnp.sum(matches * jnp.arange(enc_count * per_slot, dtype=jnp.int32)[None, :], 1)


def from_slots(received, arrival_order):
    return jnp.take(received, arrival_order, axis=0, mode="clip")


def local_body(query_raw, key_raw, value_rows, out_cotangent, image_ids, owners, gains):
    enc_count = lax.axis_size("enc")
    grp_count = lax.axis_size("grp")
    enc_rank = lax.axis_index("enc")
    per_slot = PMAX // enc_count
    feat = HEADS * HD
    group_plan = owners[0]
    own_plan = lax.dynamic_index_in_dim(group_plan, enc_rank, 0, keepdims=False)
    slot_source, _ = send_slots(own_plan, enc_count, per_slot)
    arrival_order = receive_order(group_plan, enc_rank, enc_count, per_slot)
    piece_shape = (PMAX, PIECE, feat)
    live_flags = (own_plan >= 0).astype(jnp.float32)
    live_rows = jnp.repeat(live_flags, PIECE)
    piece_of = jnp.repeat(jnp.arange(PMAX, dtype=jnp.int32), PIECE)
    d_query, d_key, d_value, gain_terms = block_grads(
        query_raw, key_raw, value_rows, out_cotangent, piece_of, image_ids, gains, live_rows
    )
    d_query = d_query.reshape(piece_shape)
    d_key = d_key.reshape(piece_shape)
    d_value = d_value.reshape(piece_shape)
    grads = jnp.concatenate((d_query, d_key, d_value), axis=-1)
    packed = jnp.take(grads, slot_source, axis=0, mode="clip")
    received = lax.all_to_all(packed, "enc", split_axis=0, concat_axis=0, tiled=True)
    mine = from_slots(received, arrival_order)
    shares = reduce_gain_terms(gain_terms, enc_count, grp_count)
    total_live = enc_count * grp_count * P_OWN * PIECE
    gain_grad = shares / math.sqrt(total_live)
    own_rows = P_OWN * PIECE
    mine = mine.reshape(own_rows, 3 * feat)
    return (
        mine[:, :feat],
        mine[:, feat : 2 * feat],
        mine[:, 2 * feat :],
        gain_grad,
    )


def solution(mesh):
    return jax.shard_map(
        local_body,
        mesh=mesh,
        in_specs=(
            P(("enc", "grp"), None),
            P(("enc", "grp"), None),
            P(("enc", "grp"), None),
            P(("enc", "grp"), None),
            P(("enc", "grp")),
            P("grp", None, None),
            P(),
        ),
        out_specs=(
            P(("enc", "grp"), None),
            P(("enc", "grp"), None),
            P(("enc", "grp"), None),
            P(None, "grp"),
        ),
        check_vma=False,
    )
```

```python
import math

import jax
import jax.numpy as jnp
from jax import lax
from jax.sharding import PartitionSpec as P


HEADS = 16
HD = 64
PIECE = 16
PMAX = 12
P_OWN = 8


epsilon = 1e-05


def normalize_rows(rows, gain_row):
    values = rows.astype(jnp.float32).reshape(rows.shape[0], HEADS, HD)
    centred = values - jnp.mean(values, -1, keepdims=True)
    inv_scale = lax.rsqrt(jnp.mean(centred * centred, -1, keepdims=True) + epsilon)
    normed = centred * inv_scale
    return (normed, inv_scale, (normed * gain_row).astype(jnp.bfloat16))


def row_norm_back(d_hat, normed, inv_scale, gain_row, live_rows):
    d_norm = d_hat * gain_row
    d_input = inv_scale * (
        d_norm
        - jnp.mean(d_norm, -1, keepdims=True)
        - normed * jnp.mean(d_norm * normed, -1, keepdims=True)
    )
    gain_term = jnp.sum(d_hat * normed * live_rows[:, None, None], 0)
    return (d_input, gain_term.reshape(-1))


def block_grads(query_rows, key_rows, value_rows, cotangent, piece_of, image_num, gains, live_rows):
    rows = query_rows.shape[0]
    three = (rows, HEADS, HD)
    gain_query = gains[0].reshape(HEADS, HD)
    gain_key = gains[1].reshape(HEADS, HD)
    q_norm, q_scale, q_hat = normalize_rows(query_rows, gain_query)
    k_norm, k_scale, k_hat = normalize_rows(key_rows, gain_key)
    values = value_rows.reshape(three)
    cot = cotangent.reshape(three)
    factor = HD ** (-0.5)
    f32 = jnp.float32
    scores = jnp.einsum("ihd,jhd->hij", q_hat, k_hat, preferred_element_type=f32) * factor
    same = (piece_of[:, None] == piece_of[None, :]) & (image_num[:, None] == image_num[None, :])
    weights = jnp.where(same[None], jnp.exp(scores), 0.0)
    probs = weights / jnp.sum(weights, -1, keepdims=True)
    probs_b = probs.astype(jnp.bfloat16)
    attended = jnp.einsum("hij,jhd->ihd", probs_b, values, preferred_element_type=f32)
    row_delta = jnp.sum(cot.astype(f32) * attended, -1)
    d_value = jnp.einsum("hij,ihd->jhd", probs_b, cot, preferred_element_type=f32)
    d_prob = jnp.einsum("ihd,jhd->hij", cot, values, preferred_element_type=f32)
    d_score = (probs * (d_prob - jnp.transpose(row_delta)[..., None]) * factor).astype(
        jnp.bfloat16
    )
    d_qhat = jnp.einsum("hij,jhd->ihd", d_score, k_hat, preferred_element_type=f32)
    d_khat = jnp.einsum("hij,ihd->jhd", d_score, q_hat, preferred_element_type=f32)
    d_query, term_query = row_norm_back(d_qhat, q_norm, q_scale, gain_query, live_rows)
    d_key, term_key = row_norm_back(d_khat, k_norm, k_scale, gain_key, live_rows)
    flat = (rows, HEADS * HD)
    return (
        d_query.reshape(flat).astype(jnp.bfloat16),
        d_key.reshape(flat).astype(jnp.bfloat16),
        d_value.reshape(flat).astype(jnp.bfloat16),
        jnp.stack([term_query, term_key]),
    )


def reduce_gain_terms(gain_terms, enc_count, grp_count):
    grp_rank = lax.axis_index("grp")
    current = gain_terms
    bit = grp_count // 2
    while bit >= 1:
        width = current.shape[1] // 2
        upper = (grp_rank // bit) % 2 == 1
        low_part = current[:, :width]
        high_part = current[:, width:]
        send = jnp.where(upper, low_part, high_part)
        keep = jnp.where(upper, high_part, low_part)
        pairs = [(i, i ^ bit) for i in range(grp_count)]
        current = keep + lax.ppermute(send, "grp", pairs)
        bit //= 2
    current = current + 0.0
    by_enc = jnp.broadcast_to(current[None], (enc_count,) + current.shape)
    by_enc = lax.all_to_all(by_enc, "enc", split_axis=0, concat_axis=0, tiled=True)
    return jnp.sum(by_enc, axis=0)


def send_slots(own_plan, enc_count, per_slot):
    owner_hit = (own_plan[:, None] == jnp.arange(enc_count, dtype=jnp.int32)[None, :]).astype(
        jnp.int32
    )
    slot_rank = jnp.sum((jnp.cumsum(owner_hit, 0) - owner_hit) * owner_hit, 1)
    slot_target = jnp.where(own_plan >= 0, own_plan * per_slot + slot_rank, -1)
    slot_ids = jnp.arange(enc_count * per_slot, dtype=jnp.int32)
    matches = (slot_target[None, :] == slot_ids[:, None]).astype(jnp.int32)
    slot_source = jnp.sum(matches * jnp.arange(PMAX, dtype=jnp.int32)[None, :], 1)
    slot_filled = jnp.sum(matches, 1) > 0
    return (slot_source, slot_filled)


def receive_order(group_plan, enc_rank, enc_count, per_slot):
    arrived = jnp.sum((group_plan == enc_rank).astype(jnp.int32), 1)
    live_slots = (
        (jnp.arange(per_slot, dtype=jnp.int32)[None, :] < arrived[:, None])
        .reshape(-1)
        .astype(jnp.int32)
    )
    live_order = jnp.cumsum(live_slots) - 1
    wanted = jnp.arange(P_OWN, dtype=jnp.int32)
    matches = ((live_order[None, :] == wanted[:, None]) & (live_slots[None, :] > 0)).astype(
        jnp.int32
    )
    return jnp.sum(matches * jnp.arange(enc_count * per_slot, dtype=jnp.int32)[None, :], 1)


def from_slots(received, arrival_order):
    return jnp.take(received, arrival_order, axis=0, mode="clip")


def local_body(query_raw, key_raw, value_rows, out_cotangent, image_ids, owners, gains):
    enc_count = lax.axis_size("enc")
    grp_count = lax.axis_size("grp")
    enc_rank = lax.axis_index("enc")
    per_slot = PMAX // enc_count
    feat = HEADS * HD
    group_plan = owners[0]
    own_plan = lax.dynamic_index_in_dim(group_plan, enc_rank, 0, keepdims=False)
    slot_source, _ = send_slots(own_plan, enc_count, per_slot)
    arrival_order = receive_order(group_plan, enc_rank, enc_count, per_slot)
    piece_shape = (PMAX, PIECE, feat)
    live_flags = (own_plan >= 0).astype(jnp.float32)
    live_rows = jnp.repeat(live_flags, PIECE)
    piece_of = jnp.repeat(jnp.arange(PMAX, dtype=jnp.int32), PIECE)
    d_query, d_key, d_value, gain_terms = block_grads(
        query_raw, key_raw, value_rows, out_cotangent, piece_of, image_ids, gains, live_rows
    )
    d_query = d_query.reshape(piece_shape)
    d_key = d_key.reshape(piece_shape)
    d_value = d_value.reshape(piece_shape)
    grads = jnp.concatenate((d_query, d_key, d_value), axis=-1)
    packed = jnp.take(grads, slot_source, axis=0, mode="clip")
    received = lax.all_to_all(packed, "enc", split_axis=0, concat_axis=0, tiled=True)
    mine = from_slots(received, arrival_order)
    shares = reduce_gain_terms(gain_terms, enc_count, grp_count)
    total_live = enc_count * grp_count * P_OWN * PIECE
    gain_grad = shares / math.sqrt(total_live)
    own_rows = P_OWN * PIECE
    mine = mine.reshape(own_rows, 3 * feat)
    return (
        mine[:, :feat],
        mine[:, feat : 2 * feat],
        mine[:, 2 * feat :],
        gain_grad,
    )


def solution(mesh):
    return jax.shard_map(
        local_body,
        mesh=mesh,
        in_specs=(
            P(("enc", "grp"), None),
            P(("enc", "grp"), None),
            P(("enc", "grp"), None),
            P(("enc", "grp"), None),
            P(("enc", "grp")),
            P("grp", None, None),
            P(),
        ),
        out_specs=(
            P(("enc", "grp"), None),
            P(("enc", "grp"), None),
            P(("enc", "grp"), None),
            P(None, "grp"),
        ),
        check_vma=False,
    )
```

```python
import math

import jax
import jax.numpy as jnp
from jax import lax
from jax.sharding import PartitionSpec as P

HEADS = 16
HD = 64
PIECE = 16
PMAX = 12
P_OWN = 8


epsilon = 1e-05


def normalize(blocks, gain_row):
    num_pieces = blocks.shape[0]
    values_four = blocks.astype(jnp.float32).reshape(num_pieces, PIECE, HEADS, HD)
    centred = values_four - jnp.mean(values_four, -1, keepdims=True)
    inv_scale = lax.rsqrt(jnp.mean(centred * centred, -1, keepdims=True) + epsilon)
    normed = centred * inv_scale
    return (normed, inv_scale, (normed * gain_row).astype(jnp.bfloat16))


def norm_back(d_hat, normed, inv_scale, gain_row, live_flags):
    d_norm = d_hat * gain_row
    d_input = inv_scale * (
        d_norm
        - jnp.mean(d_norm, -1, keepdims=True)
        - normed * jnp.mean(d_norm * normed, -1, keepdims=True)
    )
    gain_term = jnp.sum(d_hat * normed * live_flags[:, None, None, None], (0, 1))
    return (d_input, gain_term.reshape(-1))


def piece_grads(query_rows, key_rows, value_rows, cotangent, image_num, gains, live_flags):
    num_pieces = query_rows.shape[0]
    four_shape = (num_pieces, PIECE, HEADS, HD)
    gain_query = gains[0].reshape(HEADS, HD)
    gain_key = gains[1].reshape(HEADS, HD)
    q_norm, q_scale, q_hat = normalize(query_rows, gain_query)
    k_norm, k_scale, k_hat = normalize(key_rows, gain_key)
    values_four = value_rows.reshape(four_shape)
    cot_four = cotangent.reshape(four_shape)
    factor = HD ** (-0.5)
    scores = (
        jnp.einsum("bihd,bjhd->bhij", q_hat, k_hat, preferred_element_type=jnp.float32) * factor
    )
    same_image = image_num[:, None, :, None] == image_num[:, None, None, :]
    weights = jnp.where(same_image, jnp.exp(scores), 0.0)
    probs = weights / jnp.sum(weights, -1, keepdims=True)
    probs_b = probs.astype(jnp.bfloat16)
    attended = jnp.einsum(
        "bhij,bjhd->bihd", probs_b, values_four, preferred_element_type=jnp.float32
    )
    row_delta = jnp.sum(cot_four.astype(jnp.float32) * attended, -1)
    d_value = jnp.einsum(
        "bhij,bihd->bjhd", probs_b, cot_four, preferred_element_type=jnp.float32
    ).astype(jnp.bfloat16)
    d_prob = jnp.einsum(
        "bihd,bjhd->bhij", cot_four, values_four, preferred_element_type=jnp.float32
    )
    d_score = (probs * (d_prob - jnp.transpose(row_delta, (0, 2, 1))[..., None]) * factor).astype(
        jnp.bfloat16
    )
    d_qhat = jnp.einsum("bhij,bjhd->bihd", d_score, k_hat, preferred_element_type=jnp.float32)
    d_khat = jnp.einsum("bhij,bihd->bjhd", d_score, q_hat, preferred_element_type=jnp.float32)
    d_query, term_query = norm_back(d_qhat, q_norm, q_scale, gain_query, live_flags)
    d_key, term_key = norm_back(d_khat, k_norm, k_scale, gain_key, live_flags)
    flat_shape = (num_pieces, PIECE, HEADS * HD)
    return (
        d_query.reshape(flat_shape).astype(jnp.bfloat16),
        d_key.reshape(flat_shape).astype(jnp.bfloat16),
        d_value.reshape(flat_shape),
        jnp.stack([term_query, term_key]),
    )


GROUP_ROWS = 64


def normalize_rows(rows, gain_row):
    values = rows.astype(jnp.float32).reshape(rows.shape[:-1] + (HEADS, HD))
    centred = values - jnp.mean(values, -1, keepdims=True)
    inv_scale = lax.rsqrt(jnp.mean(centred * centred, -1, keepdims=True) + epsilon)
    normed = centred * inv_scale
    return (normed, inv_scale, (normed * gain_row).astype(jnp.bfloat16))


def row_norm_back(d_hat, normed, inv_scale, gain_row, live_rows):
    d_norm = d_hat * gain_row
    d_input = inv_scale * (
        d_norm
        - jnp.mean(d_norm, -1, keepdims=True)
        - normed * jnp.mean(d_norm * normed, -1, keepdims=True)
    )
    gain_term = jnp.sum(d_hat * normed * live_rows[..., None, None], (0, 1))
    return (d_input, gain_term.reshape(-1))


def block_grads(query_rows, key_rows, value_rows, cotangent, piece_of, image_num, gains, live_rows):
    rows = query_rows.shape[0]
    groups = rows // GROUP_ROWS
    grouped = (groups, GROUP_ROWS, HEADS * HD)
    four = (groups, GROUP_ROWS, HEADS, HD)
    gain_query = gains[0].reshape(HEADS, HD)
    gain_key = gains[1].reshape(HEADS, HD)
    q_norm, q_scale, q_hat = normalize_rows(query_rows.reshape(grouped), gain_query)
    k_norm, k_scale, k_hat = normalize_rows(key_rows.reshape(grouped), gain_key)
    values = value_rows.reshape(four)
    cot = cotangent.reshape(four)
    piece_of = piece_of.reshape(groups, GROUP_ROWS)
    image_num = image_num.reshape(groups, GROUP_ROWS)
    live_rows = live_rows.reshape(groups, GROUP_ROWS)
    factor = HD ** (-0.5)
    f32 = jnp.float32
    scores = jnp.einsum("gihd,gjhd->ghij", q_hat, k_hat, preferred_element_type=f32) * factor
    same = (piece_of[:, :, None] == piece_of[:, None, :]) & (
        image_num[:, :, None] == image_num[:, None, :]
    )
    weights = jnp.where(same[:, None], jnp.exp(scores), 0.0)
    probs = weights / jnp.sum(weights, -1, keepdims=True)
    probs_b = probs.astype(jnp.bfloat16)
    attended = jnp.einsum("ghij,gjhd->gihd", probs_b, values, preferred_element_type=f32)
    row_delta = jnp.sum(cot.astype(f32) * attended, -1)
    d_value = jnp.einsum("ghij,gihd->gjhd", probs_b, cot, preferred_element_type=f32)
    d_prob = jnp.einsum("gihd,gjhd->ghij", cot, values, preferred_element_type=f32)
    d_score = (
        probs * (d_prob - jnp.transpose(row_delta, (0, 2, 1))[..., None]) * factor
    ).astype(jnp.bfloat16)
    d_qhat = jnp.einsum("ghij,gjhd->gihd", d_score, k_hat, preferred_element_type=f32)
    d_khat = jnp.einsum("ghij,gihd->gjhd", d_score, q_hat, preferred_element_type=f32)
    d_query, term_query = row_norm_back(d_qhat, q_norm, q_scale, gain_query, live_rows)
    d_key, term_key = row_norm_back(d_khat, k_norm, k_scale, gain_key, live_rows)
    flat = (rows, HEADS * HD)
    return (
        d_query.reshape(flat).astype(jnp.bfloat16),
        d_key.reshape(flat).astype(jnp.bfloat16),
        d_value.reshape(flat).astype(jnp.bfloat16),
        jnp.stack([term_query, term_key]),
    )

def send_slots(own_plan, enc_count, per_slot):
    owner_hit = (own_plan[:, None] == jnp.arange(enc_count, dtype=jnp.int32)[None, :]).astype(
        jnp.int32
    )
    slot_rank = jnp.sum((jnp.cumsum(owner_hit, 0) - owner_hit) * owner_hit, 1)
    slot_target = jnp.where(own_plan >= 0, own_plan * per_slot + slot_rank, -1)
    slot_ids = jnp.arange(enc_count * per_slot, dtype=jnp.int32)
    matches = (slot_target[None, :] == slot_ids[:, None]).astype(jnp.int32)
    slot_source = jnp.sum(matches * jnp.arange(PMAX, dtype=jnp.int32)[None, :], 1)
    slot_filled = jnp.sum(matches, 1) > 0
    return (slot_source, slot_filled)


def receive_order(group_plan, enc_rank, enc_count, per_slot):
    arrived = jnp.sum((group_plan == enc_rank).astype(jnp.int32), 1)
    live_slots = (
        (jnp.arange(per_slot, dtype=jnp.int32)[None, :] < arrived[:, None])
        .reshape(-1)
        .astype(jnp.int32)
    )
    live_order = jnp.cumsum(live_slots) - 1
    wanted = jnp.arange(P_OWN, dtype=jnp.int32)
    matches = ((live_order[None, :] == wanted[:, None]) & (live_slots[None, :] > 0)).astype(
        jnp.int32
    )
    return jnp.sum(matches * jnp.arange(enc_count * per_slot, dtype=jnp.int32)[None, :], 1)


def to_slots(pieces, slot_source, slot_filled):
    taken = jnp.take(pieces, slot_source, axis=0)
    mask_shape = (slot_filled.shape[0],) + (1,) * (pieces.ndim - 1)
    taken = jnp.where(slot_filled.reshape(mask_shape), taken, jnp.zeros_like(taken))
    return taken


def from_slots(received, arrival_order):
    return jnp.take(received, arrival_order, axis=0, mode="clip")


def local(query_raw, key_raw, value_rows, out_cotangent, image_ids, owners, gains):
    enc_count = lax.axis_size("enc")
    grp_count = lax.axis_size("grp")
    enc_rank = lax.axis_index("enc")
    per_slot = PMAX // enc_count
    feat = HEADS * HD
    group_plan = owners[0]
    own_plan = lax.dynamic_index_in_dim(group_plan, enc_rank, 0, keepdims=False)
    slot_source, slot_filled = send_slots(own_plan, enc_count, per_slot)
    arrival_order = receive_order(group_plan, enc_rank, enc_count, per_slot)
    piece_shape = (PMAX, PIECE, feat)
    live_flags = (own_plan >= 0).astype(jnp.float32)
    live_rows = jnp.repeat(live_flags, PIECE)
    piece_of = jnp.repeat(jnp.arange(PMAX, dtype=jnp.int32), PIECE)
    d_query, d_key, d_value, gain_terms = block_grads(
        query_raw, key_raw, value_rows, out_cotangent, piece_of, image_ids, gains, live_rows
    )
    d_query = d_query.reshape(piece_shape)
    d_key = d_key.reshape(piece_shape)
    d_value = d_value.reshape(piece_shape)
    cols = feat // grp_count
    by_grp = jnp.transpose(gain_terms.reshape(2, grp_count, cols), (1, 0, 2))
    grp_sum = jnp.sum(
        lax.all_to_all(by_grp, "grp", split_axis=0, concat_axis=0, tiled=True), axis=0
    )
    grp_top = lax.reduce_precision(grp_sum, exponent_bits=8, mantissa_bits=7)
    grp_hi = grp_top.astype(jnp.bfloat16)
    grp_lo = (grp_sum - grp_top).astype(jnp.bfloat16)
    extra = jnp.concatenate((grp_hi, grp_lo), axis=0)
    extra = jnp.pad(extra, ((0, PIECE - 4), (0, 128 - cols)))
    extra = jnp.broadcast_to(extra[None], (PMAX, PIECE, 128))
    grads = jnp.concatenate((d_query, d_key, d_value, extra), axis=-1)
    packed = jnp.take(grads, slot_source, axis=0, mode="clip")
    received = lax.all_to_all(packed, "enc", split_axis=0, concat_axis=0, tiled=True)
    mine = from_slots(received[:, :, : 3 * feat], arrival_order)
    parts = received[:, 0:4, 3 * feat : 3 * feat + cols].astype(jnp.float32)
    shares = jnp.sum(parts[:, 0:2] + parts[:, 2:4], axis=0)
    total_live = enc_count * grp_count * P_OWN * PIECE
    gain_grad = shares / math.sqrt(total_live)
    own_rows = P_OWN * PIECE
    mine = mine.reshape(own_rows, 3 * feat)
    return (
        mine[:, :feat],
        mine[:, feat : 2 * feat],
        mine[:, 2 * feat :],
        gain_grad,
    )


def solution(mesh):
    return jax.shard_map(
        local,
        mesh=mesh,
        in_specs=(
            P(("enc", "grp"), None),
            P(("enc", "grp"), None),
            P(("enc", "grp"), None),
            P(("enc", "grp"), None),
            P(("enc", "grp")),
            P("grp", None, None),
            P(),
        ),
        out_specs=(
            P(("enc", "grp"), None),
            P(("enc", "grp"), None),
            P(("enc", "grp"), None),
            P(None, "grp"),
        ),
        check_vma=False,
    )
```

```python
import math

import jax
import jax.numpy as jnp
from jax import lax
from jax.experimental import pallas as pl
from jax.experimental.pallas import tpu as pltpu
from jax.sharding import PartitionSpec as P

HEADS = 16
HD = 64
PIECE = 16
PMAX = 12
P_OWN = 8


epsilon = 1e-05


def normalize(blocks, gain_row):
    num_pieces = blocks.shape[0]
    values_four = blocks.astype(jnp.float32).reshape(num_pieces, PIECE, HEADS, HD)
    centred = values_four - jnp.mean(values_four, -1, keepdims=True)
    inv_scale = lax.rsqrt(jnp.mean(centred * centred, -1, keepdims=True) + epsilon)
    normed = centred * inv_scale
    return (normed, inv_scale, (normed * gain_row).astype(jnp.bfloat16))


def norm_back(d_hat, normed, inv_scale, gain_row, live_flags):
    d_norm = d_hat * gain_row
    d_input = inv_scale * (
        d_norm
        - jnp.mean(d_norm, -1, keepdims=True)
        - normed * jnp.mean(d_norm * normed, -1, keepdims=True)
    )
    gain_term = jnp.sum(d_hat * normed * live_flags[:, None, None, None], (0, 1))
    return (d_input, gain_term.reshape(-1))


def piece_grads(query_rows, key_rows, value_rows, cotangent, image_num, gains, live_flags):
    num_pieces = query_rows.shape[0]
    four_shape = (num_pieces, PIECE, HEADS, HD)
    gain_query = gains[0].reshape(HEADS, HD)
    gain_key = gains[1].reshape(HEADS, HD)
    q_norm, q_scale, q_hat = normalize(query_rows, gain_query)
    k_norm, k_scale, k_hat = normalize(key_rows, gain_key)
    values_four = value_rows.reshape(four_shape)
    cot_four = cotangent.reshape(four_shape)
    factor = HD ** (-0.5)
    scores = (
        jnp.einsum("bihd,bjhd->bhij", q_hat, k_hat, preferred_element_type=jnp.float32) * factor
    )
    same_image = image_num[:, None, :, None] == image_num[:, None, None, :]
    weights = jnp.where(same_image, jnp.exp(scores), 0.0)
    probs = weights / jnp.sum(weights, -1, keepdims=True)
    probs_b = probs.astype(jnp.bfloat16)
    attended = jnp.einsum(
        "bhij,bjhd->bihd", probs_b, values_four, preferred_element_type=jnp.float32
    )
    row_delta = jnp.sum(cot_four.astype(jnp.float32) * attended, -1)
    d_value = jnp.einsum(
        "bhij,bihd->bjhd", probs_b, cot_four, preferred_element_type=jnp.float32
    ).astype(jnp.bfloat16)
    d_prob = jnp.einsum(
        "bihd,bjhd->bhij", cot_four, values_four, preferred_element_type=jnp.float32
    )
    d_score = (probs * (d_prob - jnp.transpose(row_delta, (0, 2, 1))[..., None]) * factor).astype(
        jnp.bfloat16
    )
    d_qhat = jnp.einsum("bhij,bjhd->bihd", d_score, k_hat, preferred_element_type=jnp.float32)
    d_khat = jnp.einsum("bhij,bihd->bjhd", d_score, q_hat, preferred_element_type=jnp.float32)
    d_query, term_query = norm_back(d_qhat, q_norm, q_scale, gain_query, live_flags)
    d_key, term_key = norm_back(d_khat, k_norm, k_scale, gain_key, live_flags)
    flat_shape = (num_pieces, PIECE, HEADS * HD)
    return (
        d_query.reshape(flat_shape).astype(jnp.bfloat16),
        d_key.reshape(flat_shape).astype(jnp.bfloat16),
        d_value.reshape(flat_shape),
        jnp.stack([term_query, term_key]),
    )


def normalize_rows(rows, gain_row):
    values = rows.astype(jnp.float32).reshape(rows.shape[0], HEADS, HD)
    centred = values - jnp.mean(values, -1, keepdims=True)
    inv_scale = lax.rsqrt(jnp.mean(centred * centred, -1, keepdims=True) + epsilon)
    normed = centred * inv_scale
    return (normed, inv_scale, (normed * gain_row).astype(jnp.bfloat16))


def row_norm_back(d_hat, normed, inv_scale, gain_row, live_rows):
    d_norm = d_hat * gain_row
    d_input = inv_scale * (
        d_norm
        - jnp.mean(d_norm, -1, keepdims=True)
        - normed * jnp.mean(d_norm * normed, -1, keepdims=True)
    )
    gain_term = jnp.sum(d_hat * normed * live_rows[:, None, None], 0)
    return (d_input, gain_term.reshape(-1))


def block_grads(query_rows, key_rows, value_rows, cotangent, piece_of, image_num, gains, live_rows):
    rows = query_rows.shape[0]
    three = (rows, HEADS, HD)
    gain_query = gains[0].reshape(HEADS, HD)
    gain_key = gains[1].reshape(HEADS, HD)
    q_norm, q_scale, q_hat = normalize_rows(query_rows, gain_query)
    k_norm, k_scale, k_hat = normalize_rows(key_rows, gain_key)
    values = value_rows.reshape(three)
    cot = cotangent.reshape(three)
    factor = HD ** (-0.5)
    f32 = jnp.float32
    scores = jnp.einsum("ihd,jhd->hij", q_hat, k_hat, preferred_element_type=f32) * factor
    same = (piece_of[:, None] == piece_of[None, :]) & (image_num[:, None] == image_num[None, :])
    weights = jnp.where(same[None], jnp.exp(scores), 0.0)
    probs = weights / jnp.sum(weights, -1, keepdims=True)
    probs_b = probs.astype(jnp.bfloat16)
    attended = jnp.einsum("hij,jhd->ihd", probs_b, values, preferred_element_type=f32)
    row_delta = jnp.sum(cot.astype(f32) * attended, -1)
    d_value = jnp.einsum("hij,ihd->jhd", probs_b, cot, preferred_element_type=f32)
    d_prob = jnp.einsum("ihd,jhd->hij", cot, values, preferred_element_type=f32)
    d_score = (probs * (d_prob - jnp.transpose(row_delta)[..., None]) * factor).astype(
        jnp.bfloat16
    )
    d_qhat = jnp.einsum("hij,jhd->ihd", d_score, k_hat, preferred_element_type=f32)
    d_khat = jnp.einsum("hij,ihd->jhd", d_score, q_hat, preferred_element_type=f32)
    d_query, term_query = row_norm_back(d_qhat, q_norm, q_scale, gain_query, live_rows)
    d_key, term_key = row_norm_back(d_khat, k_norm, k_scale, gain_key, live_rows)
    flat = (rows, HEADS * HD)
    return (
        d_query.reshape(flat).astype(jnp.bfloat16),
        d_key.reshape(flat).astype(jnp.bfloat16),
        d_value.reshape(flat).astype(jnp.bfloat16),
        jnp.stack([term_query, term_key]),
    )


PAD_ROWS = 256


def _norm(x, gain):
    mean = jnp.mean(x, axis=1, keepdims=True)
    centred = x - mean
    inv_scale = lax.rsqrt(jnp.mean(centred * centred, axis=1, keepdims=True) + epsilon)
    normed = centred * inv_scale
    return normed, inv_scale, (normed * gain).astype(jnp.bfloat16)


def _back(d_hat, normed, inv_scale, gain):
    d_norm = d_hat * gain
    return inv_scale * (
        d_norm
        - jnp.mean(d_norm, axis=1, keepdims=True)
        - normed * jnp.mean(d_norm * normed, axis=1, keepdims=True)
    )


def _kernel(q_ref, k_ref, v_ref, c_ref, mask_ref, live_ref, gain_ref, dq_ref, dk_ref, dv_ref, gt_ref):
    f32 = jnp.float32
    nt = (((1,), (1,)), ((), ()))
    factor = HD ** (-0.5)
    attend = mask_ref[...] > 0.5
    live = live_ref[...]
    gt_ref[...] = jnp.zeros(gt_ref.shape, f32)
    for head in range(HEADS):
        cut = slice(head * HD, (head + 1) * HD)
        gain_q = gain_ref[0:1, cut]
        gain_k = gain_ref[1:2, cut]
        q_norm, q_scale, q_hat = _norm(q_ref[:, cut].astype(f32), gain_q)
        k_norm, k_scale, k_hat = _norm(k_ref[:, cut].astype(f32), gain_k)
        values = v_ref[:, cut]
        cot = c_ref[:, cut]
        scores = lax.dot_general(q_hat, k_hat, nt, preferred_element_type=f32) * factor
        weights = jnp.where(attend, jnp.exp(scores), 0.0)
        probs = weights / jnp.sum(weights, axis=1, keepdims=True)
        probs_b = probs.astype(jnp.bfloat16)
        attended = jnp.dot(probs_b, values, preferred_element_type=f32)
        row_delta = jnp.sum(cot.astype(f32) * attended, axis=1, keepdims=True)
        probs_t = jnp.transpose(probs).astype(jnp.bfloat16)
        dv_ref[:, cut] = jnp.dot(probs_t, cot, preferred_element_type=f32).astype(jnp.bfloat16)
        d_prob = lax.dot_general(cot, values, nt, preferred_element_type=f32)
        d_score_f = probs * (d_prob - row_delta) * factor
        d_score = d_score_f.astype(jnp.bfloat16)
        d_score_t = jnp.transpose(d_score_f).astype(jnp.bfloat16)
        d_qhat = jnp.dot(d_score, k_hat, preferred_element_type=f32)
        d_khat = jnp.dot(d_score_t, q_hat, preferred_element_type=f32)
        dq_ref[:, cut] = _back(d_qhat, q_norm, q_scale, gain_q).astype(jnp.bfloat16)
        dk_ref[:, cut] = _back(d_khat, k_norm, k_scale, gain_k).astype(jnp.bfloat16)
        gt_ref[0:1, cut] = jnp.sum(d_qhat * q_norm * live, axis=0, keepdims=True)
        gt_ref[1:2, cut] = jnp.sum(d_khat * k_norm * live, axis=0, keepdims=True)


def kernel_grads(query_rows, key_rows, value_rows, cotangent, piece_of, image_num, gains, live_rows):
    rows, feat = query_rows.shape
    extra = PAD_ROWS - rows
    pad = lambda a: jnp.pad(a, ((0, extra), (0, 0)))
    piece_pad = jnp.concatenate([piece_of, -1 - jnp.arange(extra, dtype=piece_of.dtype)])
    image_pad = jnp.pad(image_num, (0, extra))
    same = (piece_pad[:, None] == piece_pad[None, :]) & (image_pad[:, None] == image_pad[None, :])
    mask = same.astype(jnp.float32)
    live = jnp.pad(live_rows, (0, extra)).reshape(PAD_ROWS, 1)
    vmem = pltpu.MemorySpace.VMEM if hasattr(pltpu, "MemorySpace") else pltpu.VMEM
    spec = pl.BlockSpec(memory_space=vmem)
    out_shape = (
        jax.ShapeDtypeStruct((PAD_ROWS, feat), jnp.bfloat16),
        jax.ShapeDtypeStruct((PAD_ROWS, feat), jnp.bfloat16),
        jax.ShapeDtypeStruct((PAD_ROWS, feat), jnp.bfloat16),
        jax.ShapeDtypeStruct((8, feat), jnp.float32),
    )
    dq, dk, dv, gt = pl.pallas_call(
        _kernel,
        out_shape=out_shape,
        in_specs=[spec] * 7,
        out_specs=(spec, spec, spec, spec),
    )(pad(query_rows), pad(key_rows), pad(value_rows), pad(cotangent), mask, live, gains)
    return dq[:rows], dk[:rows], dv[:rows], gt[0:2]


def send_slots(own_plan, enc_count, per_slot):
    owner_hit = (own_plan[:, None] == jnp.arange(enc_count, dtype=jnp.int32)[None, :]).astype(
        jnp.int32
    )
    slot_rank = jnp.sum((jnp.cumsum(owner_hit, 0) - owner_hit) * owner_hit, 1)
    slot_target = jnp.where(own_plan >= 0, own_plan * per_slot + slot_rank, -1)
    slot_ids = jnp.arange(enc_count * per_slot, dtype=jnp.int32)
    matches = (slot_target[None, :] == slot_ids[:, None]).astype(jnp.int32)
    slot_source = jnp.sum(matches * jnp.arange(PMAX, dtype=jnp.int32)[None, :], 1)
    slot_filled = jnp.sum(matches, 1) > 0
    return (slot_source, slot_filled)


def receive_order(group_plan, enc_rank, enc_count, per_slot):
    arrived = jnp.sum((group_plan == enc_rank).astype(jnp.int32), 1)
    live_slots = (
        (jnp.arange(per_slot, dtype=jnp.int32)[None, :] < arrived[:, None])
        .reshape(-1)
        .astype(jnp.int32)
    )
    live_order = jnp.cumsum(live_slots) - 1
    wanted = jnp.arange(P_OWN, dtype=jnp.int32)
    matches = ((live_order[None, :] == wanted[:, None]) & (live_slots[None, :] > 0)).astype(
        jnp.int32
    )
    return jnp.sum(matches * jnp.arange(enc_count * per_slot, dtype=jnp.int32)[None, :], 1)


def to_slots(pieces, slot_source, slot_filled):
    taken = jnp.take(pieces, slot_source, axis=0)
    mask_shape = (slot_filled.shape[0],) + (1,) * (pieces.ndim - 1)
    taken = jnp.where(slot_filled.reshape(mask_shape), taken, jnp.zeros_like(taken))
    return taken


def from_slots(received, arrival_order):
    return jnp.take(received, arrival_order, axis=0, mode="clip")


def local(query_raw, key_raw, value_rows, out_cotangent, image_ids, owners, gains):
    enc_count = lax.axis_size("enc")
    grp_count = lax.axis_size("grp")
    enc_rank = lax.axis_index("enc")
    per_slot = PMAX // enc_count
    feat = HEADS * HD
    group_plan = owners[0]
    own_plan = lax.dynamic_index_in_dim(group_plan, enc_rank, 0, keepdims=False)
    slot_source, slot_filled = send_slots(own_plan, enc_count, per_slot)
    arrival_order = receive_order(group_plan, enc_rank, enc_count, per_slot)
    piece_shape = (PMAX, PIECE, feat)
    live_flags = (own_plan >= 0).astype(jnp.float32)
    live_rows = jnp.repeat(live_flags, PIECE)
    piece_of = jnp.repeat(jnp.arange(PMAX, dtype=jnp.int32), PIECE)
    d_query, d_key, d_value, gain_terms = kernel_grads(
        query_raw, key_raw, value_rows, out_cotangent, piece_of, image_ids, gains, live_rows
    )
    d_query = d_query.reshape(piece_shape)
    d_key = d_key.reshape(piece_shape)
    d_value = d_value.reshape(piece_shape)
    cols = feat // grp_count
    by_grp = jnp.transpose(gain_terms.reshape(2, grp_count, cols), (1, 0, 2))
    grp_sum = jnp.sum(
        lax.all_to_all(by_grp, "grp", split_axis=0, concat_axis=0, tiled=True), axis=0
    )
    grp_top = lax.reduce_precision(grp_sum, exponent_bits=8, mantissa_bits=7)
    grp_hi = grp_top.astype(jnp.bfloat16)
    grp_lo = (grp_sum - grp_top).astype(jnp.bfloat16)
    extra = jnp.concatenate((grp_hi, grp_lo), axis=0)
    extra = jnp.pad(extra, ((0, PIECE - 4), (0, 128 - cols)))
    extra = jnp.broadcast_to(extra[None], (PMAX, PIECE, 128))
    grads = jnp.concatenate((d_query, d_key, d_value, extra), axis=-1)
    packed = jnp.take(grads, slot_source, axis=0, mode="clip")
    received = lax.all_to_all(packed, "enc", split_axis=0, concat_axis=0, tiled=True)
    mine = from_slots(received[:, :, : 3 * feat], arrival_order)
    parts = received[:, 0:4, 3 * feat : 3 * feat + cols].astype(jnp.float32)
    shares = jnp.sum(parts[:, 0:2] + parts[:, 2:4], axis=0)
    total_live = enc_count * grp_count * P_OWN * PIECE
    gain_grad = shares / math.sqrt(total_live)
    own_rows = P_OWN * PIECE
    mine = mine.reshape(own_rows, 3 * feat)
    return (
        mine[:, :feat],
        mine[:, feat : 2 * feat],
        mine[:, 2 * feat :],
        gain_grad,
    )


def solution(mesh):
    return jax.shard_map(
        local,
        mesh=mesh,
        in_specs=(
            P(("enc", "grp"), None),
            P(("enc", "grp"), None),
            P(("enc", "grp"), None),
            P(("enc", "grp"), None),
            P(("enc", "grp")),
            P("grp", None, None),
            P(),
        ),
        out_specs=(
            P(("enc", "grp"), None),
            P(("enc", "grp"), None),
            P(("enc", "grp"), None),
            P(None, "grp"),
        ),
        check_vma=False,
    )
```

```python
import math

import jax
import jax.numpy as jnp
from jax import lax
from jax.sharding import PartitionSpec as P


HEADS = 16
HD = 64
PIECE = 16
PMAX = 12
P_OWN = 8


epsilon = 1e-05


def normalize_rows(rows, gain_row):
    values = rows.astype(jnp.float32).reshape(rows.shape[0], HEADS, HD)
    centred = values - jnp.mean(values, -1, keepdims=True)
    inv_scale = lax.rsqrt(jnp.mean(centred * centred, -1, keepdims=True) + epsilon)
    normed = centred * inv_scale
    return (normed, inv_scale, (normed * gain_row).astype(jnp.bfloat16))


def row_norm_back(d_hat, normed, inv_scale, gain_row, live_rows):
    d_norm = d_hat * gain_row
    d_input = inv_scale * (
        d_norm
        - jnp.mean(d_norm, -1, keepdims=True)
        - normed * jnp.mean(d_norm * normed, -1, keepdims=True)
    )
    gain_term = jnp.sum(d_hat * normed * live_rows[:, None, None], 0)
    return (d_input, gain_term.reshape(-1))


def block_grads(query_rows, key_rows, value_rows, cotangent, piece_of, image_num, gains, live_rows):
    rows = query_rows.shape[0]
    three = (rows, HEADS, HD)
    gain_query = gains[0].reshape(HEADS, HD)
    gain_key = gains[1].reshape(HEADS, HD)
    q_norm, q_scale, q_hat = normalize_rows(query_rows, gain_query)
    k_norm, k_scale, k_hat = normalize_rows(key_rows, gain_key)
    values = value_rows.reshape(three)
    cot = cotangent.reshape(three)
    factor = HD ** (-0.5)
    f32 = jnp.float32
    scores = jnp.einsum("ihd,jhd->hij", q_hat, k_hat, preferred_element_type=f32) * factor
    same = (piece_of[:, None] == piece_of[None, :]) & (image_num[:, None] == image_num[None, :])
    weights = jnp.where(same[None], jnp.exp(scores), 0.0)
    probs = weights / jnp.sum(weights, -1, keepdims=True)
    probs_b = probs.astype(jnp.bfloat16)
    attended = jnp.einsum("hij,jhd->ihd", probs_b, values, preferred_element_type=f32)
    row_delta = jnp.sum(cot.astype(f32) * attended, -1)
    d_value = jnp.einsum("hij,ihd->jhd", probs_b, cot, preferred_element_type=f32)
    d_prob = jnp.einsum("ihd,jhd->hij", cot, values, preferred_element_type=f32)
    d_score = (probs * (d_prob - jnp.transpose(row_delta)[..., None]) * factor).astype(
        jnp.bfloat16
    )
    d_qhat = jnp.einsum("hij,jhd->ihd", d_score, k_hat, preferred_element_type=f32)
    d_khat = jnp.einsum("hij,ihd->jhd", d_score, q_hat, preferred_element_type=f32)
    d_query, term_query = row_norm_back(d_qhat, q_norm, q_scale, gain_query, live_rows)
    d_key, term_key = row_norm_back(d_khat, k_norm, k_scale, gain_key, live_rows)
    flat = (rows, HEADS * HD)
    return (
        d_query.reshape(flat).astype(jnp.bfloat16),
        d_key.reshape(flat).astype(jnp.bfloat16),
        d_value.reshape(flat).astype(jnp.bfloat16),
        jnp.stack([term_query, term_key]),
    )


def reduce_gain_terms(gain_terms, enc_count, grp_count):
    grp_rank = lax.axis_index("grp")
    current = gain_terms
    bit = grp_count // 2
    while bit >= 1:
        width = current.shape[1] // 2
        upper = (grp_rank // bit) % 2 == 1
        low_part = current[:, :width]
        high_part = current[:, width:]
        send = jnp.where(upper, low_part, high_part)
        keep = jnp.where(upper, high_part, low_part)
        pairs = [(i, i ^ bit) for i in range(grp_count)]
        current = keep + lax.ppermute(send, "grp", pairs)
        bit //= 2
    enc_rank = lax.axis_index("enc")
    block = enc_count // 3
    for bit in (1, 2):
        pairs = [(i, i ^ bit) for i in range(enc_count)]
        current = current + lax.ppermute(current, "enc", pairs)
    ring = [current]
    for step in (1, 2):
        pairs = [(i, (i + step * block) % enc_count) for i in range(enc_count)]
        ring.append(lax.ppermute(current, "enc", pairs))
    stacked = jnp.stack(ring)
    third = enc_rank // block
    source_order = (third - jnp.arange(3, dtype=jnp.int32)) % 3
    ordered = jnp.take(stacked, source_order, axis=0, mode="clip")
    return (ordered[0] + ordered[1]) + ordered[2]


def send_slots(own_plan, enc_count, per_slot):
    owner_hit = (own_plan[:, None] == jnp.arange(enc_count, dtype=jnp.int32)[None, :]).astype(
        jnp.int32
    )
    slot_rank = jnp.sum((jnp.cumsum(owner_hit, 0) - owner_hit) * owner_hit, 1)
    slot_target = jnp.where(own_plan >= 0, own_plan * per_slot + slot_rank, -1)
    slot_ids = jnp.arange(enc_count * per_slot, dtype=jnp.int32)
    matches = (slot_target[None, :] == slot_ids[:, None]).astype(jnp.int32)
    slot_source = jnp.sum(matches * jnp.arange(PMAX, dtype=jnp.int32)[None, :], 1)
    slot_filled = jnp.sum(matches, 1) > 0
    return (slot_source, slot_filled)


def receive_order(group_plan, enc_rank, enc_count, per_slot):
    arrived = jnp.sum((group_plan == enc_rank).astype(jnp.int32), 1)
    live_slots = (
        (jnp.arange(per_slot, dtype=jnp.int32)[None, :] < arrived[:, None])
        .reshape(-1)
        .astype(jnp.int32)
    )
    live_order = jnp.cumsum(live_slots) - 1
    wanted = jnp.arange(P_OWN, dtype=jnp.int32)
    matches = ((live_order[None, :] == wanted[:, None]) & (live_slots[None, :] > 0)).astype(
        jnp.int32
    )
    return jnp.sum(matches * jnp.arange(enc_count * per_slot, dtype=jnp.int32)[None, :], 1)


def from_slots(received, arrival_order):
    return jnp.take(received, arrival_order, axis=0, mode="clip")


def local_body(query_raw, key_raw, value_rows, out_cotangent, image_ids, owners, gains):
    enc_count = lax.axis_size("enc")
    grp_count = lax.axis_size("grp")
    enc_rank = lax.axis_index("enc")
    per_slot = PMAX // enc_count
    feat = HEADS * HD
    group_plan = owners[0]
    own_plan = lax.dynamic_index_in_dim(group_plan, enc_rank, 0, keepdims=False)
    slot_source, _ = send_slots(own_plan, enc_count, per_slot)
    arrival_order = receive_order(group_plan, enc_rank, enc_count, per_slot)
    piece_shape = (PMAX, PIECE, feat)
    live_flags = (own_plan >= 0).astype(jnp.float32)
    live_rows = jnp.repeat(live_flags, PIECE)
    piece_of = jnp.repeat(jnp.arange(PMAX, dtype=jnp.int32), PIECE)
    d_query, d_key, d_value, gain_terms = block_grads(
        query_raw, key_raw, value_rows, out_cotangent, piece_of, image_ids, gains, live_rows
    )
    d_query = d_query.reshape(piece_shape)
    d_key = d_key.reshape(piece_shape)
    d_value = d_value.reshape(piece_shape)
    grads = jnp.concatenate((d_query, d_key, d_value), axis=-1)
    packed = jnp.take(grads, slot_source, axis=0, mode="clip")
    received = lax.all_to_all(packed, "enc", split_axis=0, concat_axis=0, tiled=True)
    mine = from_slots(received, arrival_order)
    shares = reduce_gain_terms(gain_terms, enc_count, grp_count)
    total_live = enc_count * grp_count * P_OWN * PIECE
    gain_grad = shares / math.sqrt(total_live)
    own_rows = P_OWN * PIECE
    mine = mine.reshape(own_rows, 3 * feat)
    return (
        mine[:, :feat],
        mine[:, feat : 2 * feat],
        mine[:, 2 * feat :],
        gain_grad,
    )


def solution(mesh):
    return jax.shard_map(
        local_body,
        mesh=mesh,
        in_specs=(
            P(("enc", "grp"), None),
            P(("enc", "grp"), None),
            P(("enc", "grp"), None),
            P(("enc", "grp"), None),
            P(("enc", "grp")),
            P("grp", None, None),
            P(),
        ),
        out_specs=(
            P(("enc", "grp"), None),
            P(("enc", "grp"), None),
            P(("enc", "grp"), None),
            P(None, "grp"),
        ),
        check_vma=False,
    )
```

```python
import math

import jax
import jax.numpy as jnp
from jax import lax
from jax.sharding import PartitionSpec as P

HEADS = 16
HD = 64
PIECE = 16
PMAX = 12
P_OWN = 8


epsilon = 1e-05


def normalize(blocks, gain_row):
    num_pieces = blocks.shape[0]
    values_four = blocks.astype(jnp.float32).reshape(num_pieces, PIECE, HEADS, HD)
    centred = values_four - jnp.mean(values_four, -1, keepdims=True)
    inv_scale = lax.rsqrt(jnp.mean(centred * centred, -1, keepdims=True) + epsilon)
    normed = centred * inv_scale
    return (normed, inv_scale, (normed * gain_row).astype(jnp.bfloat16))


def norm_back(d_hat, normed, inv_scale, gain_row, live_flags):
    d_norm = d_hat * gain_row
    d_input = inv_scale * (
        d_norm
        - jnp.mean(d_norm, -1, keepdims=True)
        - normed * jnp.mean(d_norm * normed, -1, keepdims=True)
    )
    gain_term = jnp.sum(d_hat * normed * live_flags[:, None, None, None], (0, 1))
    return (d_input, gain_term.reshape(-1))


def piece_grads(query_rows, key_rows, value_rows, cotangent, image_num, gains, live_flags):
    num_pieces = query_rows.shape[0]
    four_shape = (num_pieces, PIECE, HEADS, HD)
    gain_query = gains[0].reshape(HEADS, HD)
    gain_key = gains[1].reshape(HEADS, HD)
    q_norm, q_scale, q_hat = normalize(query_rows, gain_query)
    k_norm, k_scale, k_hat = normalize(key_rows, gain_key)
    values_four = value_rows.reshape(four_shape)
    cot_four = cotangent.reshape(four_shape)
    factor = HD ** (-0.5)
    scores = (
        jnp.einsum("bihd,bjhd->bhij", q_hat, k_hat, preferred_element_type=jnp.float32) * factor
    )
    same_image = image_num[:, None, :, None] == image_num[:, None, None, :]
    weights = jnp.where(same_image, jnp.exp(scores), 0.0)
    probs = weights / jnp.sum(weights, -1, keepdims=True)
    probs_b = probs.astype(jnp.bfloat16)
    attended = jnp.einsum(
        "bhij,bjhd->bihd", probs_b, values_four, preferred_element_type=jnp.float32
    )
    row_delta = jnp.sum(cot_four.astype(jnp.float32) * attended, -1)
    d_value = jnp.einsum(
        "bhij,bihd->bjhd", probs_b, cot_four, preferred_element_type=jnp.float32
    ).astype(jnp.bfloat16)
    d_prob = jnp.einsum(
        "bihd,bjhd->bhij", cot_four, values_four, preferred_element_type=jnp.float32
    )
    d_score = (probs * (d_prob - jnp.transpose(row_delta, (0, 2, 1))[..., None]) * factor).astype(
        jnp.bfloat16
    )
    d_qhat = jnp.einsum("bhij,bjhd->bihd", d_score, k_hat, preferred_element_type=jnp.float32)
    d_khat = jnp.einsum("bhij,bihd->bjhd", d_score, q_hat, preferred_element_type=jnp.float32)
    d_query, term_query = norm_back(d_qhat, q_norm, q_scale, gain_query, live_flags)
    d_key, term_key = norm_back(d_khat, k_norm, k_scale, gain_key, live_flags)
    flat_shape = (num_pieces, PIECE, HEADS * HD)
    return (
        d_query.reshape(flat_shape).astype(jnp.bfloat16),
        d_key.reshape(flat_shape).astype(jnp.bfloat16),
        d_value.reshape(flat_shape),
        jnp.stack([term_query, term_key]),
    )


def normalize_rows(rows, gain_row):
    values = rows.astype(jnp.float32)
    centred = values - jnp.mean(values, -1, keepdims=True)
    inv_scale = lax.rsqrt(jnp.mean(centred * centred, -1, keepdims=True) + epsilon)
    normed = centred * inv_scale
    return (normed, inv_scale, (normed * gain_row[:, None, :]).astype(jnp.bfloat16))


def row_norm_back(d_hat, normed, inv_scale, gain_row, live_rows):
    d_norm = d_hat * gain_row[:, None, :]
    d_input = inv_scale * (
        d_norm
        - jnp.mean(d_norm, -1, keepdims=True)
        - normed * jnp.mean(d_norm * normed, -1, keepdims=True)
    )
    gain_term = jnp.sum(d_hat * normed * live_rows[None, :, None], 1)
    return (d_input, gain_term.reshape(-1))


def head_major(rows):
    return jnp.transpose(rows.reshape(rows.shape[0], HEADS, HD), (1, 0, 2))


def row_major(heads):
    return jnp.transpose(heads, (1, 0, 2)).reshape(heads.shape[1], HEADS * HD)


def block_grads(query_rows, key_rows, value_rows, cotangent, piece_of, image_num, gains, live_rows):
    gain_query = gains[0].reshape(HEADS, HD)
    gain_key = gains[1].reshape(HEADS, HD)
    q_norm, q_scale, q_hat = normalize_rows(head_major(query_rows), gain_query)
    k_norm, k_scale, k_hat = normalize_rows(head_major(key_rows), gain_key)
    values = head_major(value_rows)
    cot = head_major(cotangent)
    factor = HD ** (-0.5)
    f32 = jnp.float32
    scores = jnp.einsum("hid,hjd->hij", q_hat, k_hat, preferred_element_type=f32) * factor
    same = (piece_of[:, None] == piece_of[None, :]) & (image_num[:, None] == image_num[None, :])
    weights = jnp.where(same[None], jnp.exp(scores), 0.0)
    probs = weights / jnp.sum(weights, -1, keepdims=True)
    probs_b = probs.astype(jnp.bfloat16)
    attended = jnp.einsum("hij,hjd->hid", probs_b, values, preferred_element_type=f32)
    row_delta = jnp.sum(cot.astype(f32) * attended, -1)
    d_value = jnp.einsum("hij,hid->hjd", probs_b, cot, preferred_element_type=f32)
    d_prob = jnp.einsum("hid,hjd->hij", cot, values, preferred_element_type=f32)
    d_score = (probs * (d_prob - row_delta[..., None]) * factor).astype(jnp.bfloat16)
    d_qhat = jnp.einsum("hij,hjd->hid", d_score, k_hat, preferred_element_type=f32)
    d_khat = jnp.einsum("hij,hid->hjd", d_score, q_hat, preferred_element_type=f32)
    d_query, term_query = row_norm_back(d_qhat, q_norm, q_scale, gain_query, live_rows)
    d_key, term_key = row_norm_back(d_khat, k_norm, k_scale, gain_key, live_rows)
    return (
        row_major(d_query.astype(jnp.bfloat16)),
        row_major(d_key.astype(jnp.bfloat16)),
        row_major(d_value.astype(jnp.bfloat16)),
        jnp.stack([term_query, term_key]),
    )

def send_slots(own_plan, enc_count, per_slot):
    owner_hit = (own_plan[:, None] == jnp.arange(enc_count, dtype=jnp.int32)[None, :]).astype(
        jnp.int32
    )
    slot_rank = jnp.sum((jnp.cumsum(owner_hit, 0) - owner_hit) * owner_hit, 1)
    slot_target = jnp.where(own_plan >= 0, own_plan * per_slot + slot_rank, -1)
    slot_ids = jnp.arange(enc_count * per_slot, dtype=jnp.int32)
    matches = (slot_target[None, :] == slot_ids[:, None]).astype(jnp.int32)
    slot_source = jnp.sum(matches * jnp.arange(PMAX, dtype=jnp.int32)[None, :], 1)
    slot_filled = jnp.sum(matches, 1) > 0
    return (slot_source, slot_filled)


def receive_order(group_plan, enc_rank, enc_count, per_slot):
    arrived = jnp.sum((group_plan == enc_rank).astype(jnp.int32), 1)
    live_slots = (
        (jnp.arange(per_slot, dtype=jnp.int32)[None, :] < arrived[:, None])
        .reshape(-1)
        .astype(jnp.int32)
    )
    live_order = jnp.cumsum(live_slots) - 1
    wanted = jnp.arange(P_OWN, dtype=jnp.int32)
    matches = ((live_order[None, :] == wanted[:, None]) & (live_slots[None, :] > 0)).astype(
        jnp.int32
    )
    return jnp.sum(matches * jnp.arange(enc_count * per_slot, dtype=jnp.int32)[None, :], 1)


def to_slots(pieces, slot_source, slot_filled):
    taken = jnp.take(pieces, slot_source, axis=0)
    mask_shape = (slot_filled.shape[0],) + (1,) * (pieces.ndim - 1)
    taken = jnp.where(slot_filled.reshape(mask_shape), taken, jnp.zeros_like(taken))
    return taken


def from_slots(received, arrival_order):
    return jnp.take(received, arrival_order, axis=0, mode="clip")


def local(query_raw, key_raw, value_rows, out_cotangent, image_ids, owners, gains):
    enc_count = lax.axis_size("enc")
    grp_count = lax.axis_size("grp")
    enc_rank = lax.axis_index("enc")
    per_slot = PMAX // enc_count
    feat = HEADS * HD
    group_plan = owners[0]
    own_plan = lax.dynamic_index_in_dim(group_plan, enc_rank, 0, keepdims=False)
    slot_source, slot_filled = send_slots(own_plan, enc_count, per_slot)
    arrival_order = receive_order(group_plan, enc_rank, enc_count, per_slot)
    piece_shape = (PMAX, PIECE, feat)
    live_flags = (own_plan >= 0).astype(jnp.float32)
    live_rows = jnp.repeat(live_flags, PIECE)
    piece_of = jnp.repeat(jnp.arange(PMAX, dtype=jnp.int32), PIECE)
    d_query, d_key, d_value, gain_terms = block_grads(
        query_raw, key_raw, value_rows, out_cotangent, piece_of, image_ids, gains, live_rows
    )
    d_query = d_query.reshape(piece_shape)
    d_key = d_key.reshape(piece_shape)
    d_value = d_value.reshape(piece_shape)
    cols = feat // grp_count
    by_grp = jnp.transpose(gain_terms.reshape(2, grp_count, cols), (1, 0, 2))
    grp_sum = jnp.sum(
        lax.all_to_all(by_grp, "grp", split_axis=0, concat_axis=0, tiled=True), axis=0
    )
    grp_top = lax.reduce_precision(grp_sum, exponent_bits=8, mantissa_bits=7)
    grp_hi = grp_top.astype(jnp.bfloat16)
    grp_lo = (grp_sum - grp_top).astype(jnp.bfloat16)
    extra = jnp.concatenate((grp_hi, grp_lo), axis=0)
    extra = jnp.pad(extra, ((0, PIECE - 4), (0, 128 - cols)))
    extra = jnp.broadcast_to(extra[None], (PMAX, PIECE, 128))
    grads = jnp.concatenate((d_query, d_key, d_value, extra), axis=-1)
    packed = jnp.take(grads, slot_source, axis=0, mode="clip")
    received = lax.all_to_all(packed, "enc", split_axis=0, concat_axis=0, tiled=True)
    mine = from_slots(received[:, :, : 3 * feat], arrival_order)
    parts = received[:, 0:4, 3 * feat : 3 * feat + cols].astype(jnp.float32)
    shares = jnp.sum(parts[:, 0:2] + parts[:, 2:4], axis=0)
    total_live = enc_count * grp_count * P_OWN * PIECE
    gain_grad = shares / math.sqrt(total_live)
    own_rows = P_OWN * PIECE
    mine = mine.reshape(own_rows, 3 * feat)
    return (
        mine[:, :feat],
        mine[:, feat : 2 * feat],
        mine[:, 2 * feat :],
        gain_grad,
    )


def solution(mesh):
    return jax.shard_map(
        local,
        mesh=mesh,
        in_specs=(
            P(("enc", "grp"), None),
            P(("enc", "grp"), None),
            P(("enc", "grp"), None),
            P(("enc", "grp"), None),
            P(("enc", "grp")),
            P("grp", None, None),
            P(),
        ),
        out_specs=(
            P(("enc", "grp"), None),
            P(("enc", "grp"), None),
            P(("enc", "grp"), None),
            P(None, "grp"),
        ),
        check_vma=False,
    )
```

```python
import math

import jax
import jax.numpy as jnp
from jax import lax
from jax.sharding import PartitionSpec as P

HEADS = 16
HD = 64
PIECE = 16
PMAX = 12
P_OWN = 8


epsilon = 1e-05


def normalize(blocks, gain_row):
    num_pieces = blocks.shape[0]
    values_four = blocks.astype(jnp.float32).reshape(num_pieces, PIECE, HEADS, HD)
    centred = values_four - jnp.mean(values_four, -1, keepdims=True)
    inv_scale = lax.rsqrt(jnp.mean(centred * centred, -1, keepdims=True) + epsilon)
    normed = centred * inv_scale
    return (normed, inv_scale, (normed * gain_row).astype(jnp.bfloat16))


def norm_back(d_hat, normed, inv_scale, gain_row, live_flags):
    d_norm = d_hat * gain_row
    d_input = inv_scale * (
        d_norm
        - jnp.mean(d_norm, -1, keepdims=True)
        - normed * jnp.mean(d_norm * normed, -1, keepdims=True)
    )
    gain_term = jnp.sum(d_hat * normed * live_flags[:, None, None, None], (0, 1))
    return (d_input, gain_term.reshape(-1))


def piece_grads(query_rows, key_rows, value_rows, cotangent, image_num, gains, live_flags):
    num_pieces = query_rows.shape[0]
    four_shape = (num_pieces, PIECE, HEADS, HD)
    gain_query = gains[0].reshape(HEADS, HD)
    gain_key = gains[1].reshape(HEADS, HD)
    q_norm, q_scale, q_hat = normalize(query_rows, gain_query)
    k_norm, k_scale, k_hat = normalize(key_rows, gain_key)
    values_four = value_rows.reshape(four_shape)
    cot_four = cotangent.reshape(four_shape)
    factor = HD ** (-0.5)
    scores = (
        jnp.einsum("bihd,bjhd->bhij", q_hat, k_hat, preferred_element_type=jnp.float32) * factor
    )
    same_image = image_num[:, None, :, None] == image_num[:, None, None, :]
    weights = jnp.where(same_image, jnp.exp(scores), 0.0)
    probs = weights / jnp.sum(weights, -1, keepdims=True)
    probs_b = probs.astype(jnp.bfloat16)
    attended = jnp.einsum(
        "bhij,bjhd->bihd", probs_b, values_four, preferred_element_type=jnp.float32
    )
    row_delta = jnp.sum(cot_four.astype(jnp.float32) * attended, -1)
    d_value = jnp.einsum(
        "bhij,bihd->bjhd", probs_b, cot_four, preferred_element_type=jnp.float32
    ).astype(jnp.bfloat16)
    d_prob = jnp.einsum(
        "bihd,bjhd->bhij", cot_four, values_four, preferred_element_type=jnp.float32
    )
    d_score = (probs * (d_prob - jnp.transpose(row_delta, (0, 2, 1))[..., None]) * factor).astype(
        jnp.bfloat16
    )
    d_qhat = jnp.einsum("bhij,bjhd->bihd", d_score, k_hat, preferred_element_type=jnp.float32)
    d_khat = jnp.einsum("bhij,bihd->bjhd", d_score, q_hat, preferred_element_type=jnp.float32)
    d_query, term_query = norm_back(d_qhat, q_norm, q_scale, gain_query, live_flags)
    d_key, term_key = norm_back(d_khat, k_norm, k_scale, gain_key, live_flags)
    flat_shape = (num_pieces, PIECE, HEADS * HD)
    return (
        d_query.reshape(flat_shape).astype(jnp.bfloat16),
        d_key.reshape(flat_shape).astype(jnp.bfloat16),
        d_value.reshape(flat_shape),
        jnp.stack([term_query, term_key]),
    )


def normalize_rows(rows, gain_row):
    values = rows.astype(jnp.float32).reshape(rows.shape[0], HEADS, HD)
    centred = values - jnp.mean(values, -1, keepdims=True)
    inv_scale = lax.rsqrt(jnp.mean(centred * centred, -1, keepdims=True) + epsilon)
    normed = centred * inv_scale
    return (normed, inv_scale, (normed * gain_row).astype(jnp.bfloat16))


def row_norm_back(d_hat, normed, inv_scale, gain_row, live_rows):
    d_norm = d_hat * gain_row
    d_input = inv_scale * (
        d_norm
        - jnp.mean(d_norm, -1, keepdims=True)
        - normed * jnp.mean(d_norm * normed, -1, keepdims=True)
    )
    gain_term = jnp.sum(d_hat * normed * live_rows[:, None, None], 0)
    return (d_input, gain_term.reshape(-1))


def block_grads(query_rows, key_rows, value_rows, cotangent, piece_of, image_num, gains, live_rows):
    rows = query_rows.shape[0]
    three = (rows, HEADS, HD)
    gain_query = gains[0].reshape(HEADS, HD)
    gain_key = gains[1].reshape(HEADS, HD)
    q_norm, q_scale, q_hat = normalize_rows(query_rows, gain_query)
    k_norm, k_scale, k_hat = normalize_rows(key_rows, gain_key)
    values = value_rows.reshape(three)
    cot = cotangent.reshape(three)
    factor = HD ** (-0.5)
    f32 = jnp.float32
    scores = jnp.einsum("ihd,jhd->hij", q_hat, k_hat, preferred_element_type=f32) * factor
    same = (piece_of[:, None] == piece_of[None, :]) & (image_num[:, None] == image_num[None, :])
    weights = jnp.where(same[None], jnp.exp(scores), 0.0)
    probs = weights / jnp.sum(weights, -1, keepdims=True)
    probs_b = probs.astype(jnp.bfloat16)
    attended = jnp.einsum("hij,jhd->ihd", probs_b, values, preferred_element_type=f32)
    row_delta = jnp.sum(cot.astype(f32) * attended, -1)
    d_value = jnp.einsum("hij,ihd->jhd", probs_b, cot, preferred_element_type=f32)
    d_prob = jnp.einsum("ihd,jhd->hij", cot, values, preferred_element_type=f32)
    d_score = (probs * (d_prob - jnp.transpose(row_delta)[..., None]) * factor).astype(
        jnp.bfloat16
    )
    d_qhat = jnp.einsum("hij,jhd->ihd", d_score, k_hat, preferred_element_type=f32)
    d_khat = jnp.einsum("hij,ihd->jhd", d_score, q_hat, preferred_element_type=f32)
    d_query, term_query = row_norm_back(d_qhat, q_norm, q_scale, gain_query, live_rows)
    d_key, term_key = row_norm_back(d_khat, k_norm, k_scale, gain_key, live_rows)
    flat = (rows, HEADS * HD)
    return (
        d_query.reshape(flat).astype(jnp.bfloat16),
        d_key.reshape(flat).astype(jnp.bfloat16),
        d_value.reshape(flat).astype(jnp.bfloat16),
        jnp.stack([term_query, term_key]),
    )


def send_slots(own_plan, enc_count, per_slot):
    owner_hit = (own_plan[:, None] == jnp.arange(enc_count, dtype=jnp.int32)[None, :]).astype(
        jnp.int32
    )
    slot_rank = jnp.sum((jnp.cumsum(owner_hit, 0) - owner_hit) * owner_hit, 1)
    slot_target = jnp.where(own_plan >= 0, own_plan * per_slot + slot_rank, -1)
    slot_ids = jnp.arange(enc_count * per_slot, dtype=jnp.int32)
    matches = (slot_target[None, :] == slot_ids[:, None]).astype(jnp.int32)
    slot_source = jnp.sum(matches * jnp.arange(PMAX, dtype=jnp.int32)[None, :], 1)
    slot_filled = jnp.sum(matches, 1) > 0
    return (slot_source, slot_filled)


def receive_order(group_plan, enc_rank, enc_count, per_slot):
    arrived = jnp.sum((group_plan == enc_rank).astype(jnp.int32), 1)
    live_slots = (
        (jnp.arange(per_slot, dtype=jnp.int32)[None, :] < arrived[:, None])
        .reshape(-1)
        .astype(jnp.int32)
    )
    live_order = jnp.cumsum(live_slots) - 1
    wanted = jnp.arange(P_OWN, dtype=jnp.int32)
    matches = ((live_order[None, :] == wanted[:, None]) & (live_slots[None, :] > 0)).astype(
        jnp.int32
    )
    return jnp.sum(matches * jnp.arange(enc_count * per_slot, dtype=jnp.int32)[None, :], 1)


def to_slots(pieces, slot_source, slot_filled):
    taken = jnp.take(pieces, slot_source, axis=0)
    mask_shape = (slot_filled.shape[0],) + (1,) * (pieces.ndim - 1)
    taken = jnp.where(slot_filled.reshape(mask_shape), taken, jnp.zeros_like(taken))
    return taken


def from_slots(received, arrival_order):
    return jnp.take(received, arrival_order, axis=0, mode="clip")


def local(query_raw, key_raw, value_rows, out_cotangent, image_ids, owners, gains):
    enc_count = lax.axis_size("enc")
    grp_count = lax.axis_size("grp")
    enc_rank = lax.axis_index("enc")
    per_slot = PMAX // enc_count
    feat = HEADS * HD
    group_plan = owners[0]
    own_plan = lax.dynamic_index_in_dim(group_plan, enc_rank, 0, keepdims=False)
    slot_source, slot_filled = send_slots(own_plan, enc_count, per_slot)
    arrival_order = receive_order(group_plan, enc_rank, enc_count, per_slot)
    piece_shape = (PMAX, PIECE, feat)
    live_flags = (own_plan >= 0).astype(jnp.float32)
    live_rows = jnp.repeat(live_flags, PIECE)
    piece_of = jnp.repeat(jnp.arange(PMAX, dtype=jnp.int32), PIECE)
    d_query, d_key, d_value, gain_terms = block_grads(
        query_raw, key_raw, value_rows, out_cotangent, piece_of, image_ids, gains, live_rows
    )
    d_query = d_query.reshape(piece_shape)
    d_key = d_key.reshape(piece_shape)
    d_value = d_value.reshape(piece_shape)
    cols = feat // grp_count
    term_top = lax.reduce_precision(gain_terms, exponent_bits=8, mantissa_bits=7)
    term_hi = term_top.astype(jnp.bfloat16)
    term_lo = (gain_terms - term_top).astype(jnp.bfloat16)
    extra = jnp.concatenate((term_hi, term_lo), axis=0).reshape(PIECE, 256)
    extra = jnp.broadcast_to(extra[None], (PMAX, PIECE, 256))
    grads = jnp.concatenate((d_query, d_key, d_value, extra), axis=-1)
    packed = jnp.take(grads, slot_source, axis=0, mode="clip")
    received = lax.all_to_all(packed, "enc", split_axis=0, concat_axis=0, tiled=True)
    mine = from_slots(received[:, :, : 3 * feat], arrival_order)
    parts = received[:, :, 3 * feat :].astype(jnp.float32).reshape(enc_count, 4, feat)
    group_total = jnp.sum(parts[:, 0:2] + parts[:, 2:4], axis=0)
    by_grp = jnp.transpose(group_total.reshape(2, grp_count, cols), (1, 0, 2))
    shares = jnp.sum(
        lax.all_to_all(by_grp, "grp", split_axis=0, concat_axis=0, tiled=True), axis=0
    )
    total_live = enc_count * grp_count * P_OWN * PIECE
    gain_grad = shares / math.sqrt(total_live)
    own_rows = P_OWN * PIECE
    mine = mine.reshape(own_rows, 3 * feat)
    return (
        mine[:, :feat],
        mine[:, feat : 2 * feat],
        mine[:, 2 * feat :],
        gain_grad,
    )


def solution(mesh):
    return jax.shard_map(
        local,
        mesh=mesh,
        in_specs=(
            P(("enc", "grp"), None),
            P(("enc", "grp"), None),
            P(("enc", "grp"), None),
            P(("enc", "grp"), None),
            P(("enc", "grp")),
            P("grp", None, None),
            P(),
        ),
        out_specs=(
            P(("enc", "grp"), None),
            P(("enc", "grp"), None),
            P(("enc", "grp"), None),
            P(None, "grp"),
        ),
        check_vma=False,
    )
```

```python
import math

import jax
import jax.numpy as jnp
from jax import lax
from jax.sharding import PartitionSpec as P

HEADS = 16
HD = 64
PIECE = 16
PMAX = 12
P_OWN = 8


epsilon = 1e-05


def normalize(blocks, gain_row):
    num_pieces = blocks.shape[0]
    values_four = blocks.astype(jnp.float32).reshape(num_pieces, PIECE, HEADS, HD)
    centred = values_four - jnp.mean(values_four, -1, keepdims=True)
    inv_scale = lax.rsqrt(jnp.mean(centred * centred, -1, keepdims=True) + epsilon)
    normed = centred * inv_scale
    return (normed, inv_scale, (normed * gain_row).astype(jnp.bfloat16))


def norm_back(d_hat, normed, inv_scale, gain_row, live_flags):
    d_norm = d_hat * gain_row
    d_input = inv_scale * (
        d_norm
        - jnp.mean(d_norm, -1, keepdims=True)
        - normed * jnp.mean(d_norm * normed, -1, keepdims=True)
    )
    gain_term = jnp.sum(d_hat * normed * live_flags[:, None, None, None], (0, 1))
    return (d_input, gain_term.reshape(-1))


def piece_grads(query_rows, key_rows, value_rows, cotangent, image_num, gains, live_flags):
    num_pieces = query_rows.shape[0]
    four_shape = (num_pieces, PIECE, HEADS, HD)
    gain_query = gains[0].reshape(HEADS, HD)
    gain_key = gains[1].reshape(HEADS, HD)
    q_norm, q_scale, q_hat = normalize(query_rows, gain_query)
    k_norm, k_scale, k_hat = normalize(key_rows, gain_key)
    values_four = value_rows.reshape(four_shape)
    cot_four = cotangent.reshape(four_shape)
    factor = HD ** (-0.5)
    scores = (
        jnp.einsum("bihd,bjhd->bhij", q_hat, k_hat, preferred_element_type=jnp.float32) * factor
    )
    same_image = image_num[:, None, :, None] == image_num[:, None, None, :]
    weights = jnp.where(same_image, jnp.exp(scores), 0.0)
    probs = weights / jnp.sum(weights, -1, keepdims=True)
    probs_b = probs.astype(jnp.bfloat16)
    attended = jnp.einsum(
        "bhij,bjhd->bihd", probs_b, values_four, preferred_element_type=jnp.float32
    )
    row_delta = jnp.sum(cot_four.astype(jnp.float32) * attended, -1)
    d_value = jnp.einsum(
        "bhij,bihd->bjhd", probs_b, cot_four, preferred_element_type=jnp.float32
    ).astype(jnp.bfloat16)
    d_prob = jnp.einsum(
        "bihd,bjhd->bhij", cot_four, values_four, preferred_element_type=jnp.float32
    )
    d_score = (probs * (d_prob - jnp.transpose(row_delta, (0, 2, 1))[..., None]) * factor).astype(
        jnp.bfloat16
    )
    d_qhat = jnp.einsum("bhij,bjhd->bihd", d_score, k_hat, preferred_element_type=jnp.float32)
    d_khat = jnp.einsum("bhij,bihd->bjhd", d_score, q_hat, preferred_element_type=jnp.float32)
    d_query, term_query = norm_back(d_qhat, q_norm, q_scale, gain_query, live_flags)
    d_key, term_key = norm_back(d_khat, k_norm, k_scale, gain_key, live_flags)
    flat_shape = (num_pieces, PIECE, HEADS * HD)
    return (
        d_query.reshape(flat_shape).astype(jnp.bfloat16),
        d_key.reshape(flat_shape).astype(jnp.bfloat16),
        d_value.reshape(flat_shape),
        jnp.stack([term_query, term_key]),
    )


def normalize_rows(rows, gain_row):
    values = rows.astype(jnp.float32).reshape(rows.shape[0], HEADS, HD)
    centred = values - jnp.mean(values, -1, keepdims=True)
    inv_scale = lax.rsqrt(jnp.mean(centred * centred, -1, keepdims=True) + epsilon)
    normed = centred * inv_scale
    return (normed, inv_scale, (normed * gain_row).astype(jnp.bfloat16))


def row_norm_back(d_hat, normed, inv_scale, gain_row, live_rows):
    d_norm = d_hat * gain_row
    d_input = inv_scale * (
        d_norm
        - jnp.mean(d_norm, -1, keepdims=True)
        - normed * jnp.mean(d_norm * normed, -1, keepdims=True)
    )
    gain_term = jnp.sum(d_hat * normed * live_rows[:, None, None], 0)
    return (d_input, gain_term.reshape(-1))


def block_grads(query_rows, key_rows, value_rows, cotangent, piece_of, image_num, gains, live_rows):
    rows = query_rows.shape[0]
    three = (rows, HEADS, HD)
    gain_query = gains[0].reshape(HEADS, HD)
    gain_key = gains[1].reshape(HEADS, HD)
    q_norm, q_scale, q_hat = normalize_rows(query_rows, gain_query)
    k_norm, k_scale, k_hat = normalize_rows(key_rows, gain_key)
    values = value_rows.reshape(three)
    cot = cotangent.reshape(three)
    factor = HD ** (-0.5)
    f32 = jnp.float32
    scores = jnp.einsum("ihd,jhd->hij", q_hat, k_hat, preferred_element_type=f32) * factor
    same = (piece_of[:, None] == piece_of[None, :]) & (image_num[:, None] == image_num[None, :])
    weights = jnp.where(same[None], jnp.exp(scores), 0.0)
    probs = weights / jnp.sum(weights, -1, keepdims=True)
    probs_b = probs.astype(jnp.bfloat16)
    attended = jnp.einsum("hij,jhd->ihd", probs_b, values, preferred_element_type=f32)
    row_delta = jnp.sum(cot.astype(f32) * attended, -1)
    d_value = jnp.einsum("hij,ihd->jhd", probs_b, cot, preferred_element_type=f32)
    d_prob = jnp.einsum("ihd,jhd->hij", cot, values, preferred_element_type=f32)
    d_score = (probs * (d_prob - jnp.transpose(row_delta)[..., None]) * factor).astype(
        jnp.bfloat16
    )
    d_qhat = jnp.einsum("hij,jhd->ihd", d_score, k_hat, preferred_element_type=f32)
    d_khat = jnp.einsum("hij,ihd->jhd", d_score, q_hat, preferred_element_type=f32)
    d_query, term_query = row_norm_back(d_qhat, q_norm, q_scale, gain_query, live_rows)
    d_key, term_key = row_norm_back(d_khat, k_norm, k_scale, gain_key, live_rows)
    flat = (rows, HEADS * HD)
    return (
        d_query.reshape(flat).astype(jnp.bfloat16),
        d_key.reshape(flat).astype(jnp.bfloat16),
        d_value.reshape(flat).astype(jnp.bfloat16),
        jnp.stack([term_query, term_key]),
    )


def send_slots(own_plan, enc_count, per_slot):
    owner_hit = (own_plan[:, None] == jnp.arange(enc_count, dtype=jnp.int32)[None, :]).astype(
        jnp.int32
    )
    slot_rank = jnp.sum((jnp.cumsum(owner_hit, 0) - owner_hit) * owner_hit, 1)
    slot_target = jnp.where(own_plan >= 0, own_plan * per_slot + slot_rank, -1)
    slot_ids = jnp.arange(enc_count * per_slot, dtype=jnp.int32)
    matches = (slot_target[None, :] == slot_ids[:, None]).astype(jnp.int32)
    slot_source = jnp.sum(matches * jnp.arange(PMAX, dtype=jnp.int32)[None, :], 1)
    slot_filled = jnp.sum(matches, 1) > 0
    return (slot_source, slot_filled)


def receive_order(group_plan, enc_rank, enc_count, per_slot):
    arrived = jnp.sum((group_plan == enc_rank).astype(jnp.int32), 1)
    live_slots = (
        (jnp.arange(per_slot, dtype=jnp.int32)[None, :] < arrived[:, None])
        .reshape(-1)
        .astype(jnp.int32)
    )
    live_order = jnp.cumsum(live_slots) - 1
    wanted = jnp.arange(P_OWN, dtype=jnp.int32)
    matches = ((live_order[None, :] == wanted[:, None]) & (live_slots[None, :] > 0)).astype(
        jnp.int32
    )
    return jnp.sum(matches * jnp.arange(enc_count * per_slot, dtype=jnp.int32)[None, :], 1)


def to_slots(pieces, slot_source, slot_filled):
    taken = jnp.take(pieces, slot_source, axis=0)
    mask_shape = (slot_filled.shape[0],) + (1,) * (pieces.ndim - 1)
    taken = jnp.where(slot_filled.reshape(mask_shape), taken, jnp.zeros_like(taken))
    return taken


def from_slots(received, arrival_order):
    return received.at[arrival_order].get(mode="promise_in_bounds")


def local(query_raw, key_raw, value_rows, out_cotangent, image_ids, owners, gains):
    enc_count = lax.axis_size("enc")
    grp_count = lax.axis_size("grp")
    enc_rank = lax.axis_index("enc")
    per_slot = PMAX // enc_count
    feat = HEADS * HD
    group_plan = owners[0]
    own_plan = lax.dynamic_index_in_dim(group_plan, enc_rank, 0, keepdims=False)
    slot_source, slot_filled = send_slots(own_plan, enc_count, per_slot)
    arrival_order = receive_order(group_plan, enc_rank, enc_count, per_slot)
    piece_shape = (PMAX, PIECE, feat)
    live_flags = (own_plan >= 0).astype(jnp.float32)
    live_rows = jnp.repeat(live_flags, PIECE)
    piece_of = jnp.repeat(jnp.arange(PMAX, dtype=jnp.int32), PIECE)
    d_query, d_key, d_value, gain_terms = block_grads(
        query_raw, key_raw, value_rows, out_cotangent, piece_of, image_ids, gains, live_rows
    )
    d_query = d_query.reshape(piece_shape)
    d_key = d_key.reshape(piece_shape)
    d_value = d_value.reshape(piece_shape)
    cols = feat // grp_count
    by_grp = jnp.transpose(gain_terms.reshape(2, grp_count, cols), (1, 0, 2))
    grp_sum = jnp.sum(
        lax.all_to_all(by_grp, "grp", split_axis=0, concat_axis=0, tiled=True), axis=0
    )
    grp_top = lax.reduce_precision(grp_sum, exponent_bits=8, mantissa_bits=7)
    grp_hi = grp_top.astype(jnp.bfloat16)
    grp_lo = (grp_sum - grp_top).astype(jnp.bfloat16)
    extra = jnp.concatenate((grp_hi, grp_lo), axis=0)
    extra = jnp.pad(extra, ((0, PIECE - 4), (0, 128 - cols)))
    extra = jnp.broadcast_to(extra[None], (PMAX, PIECE, 128))
    grads = jnp.concatenate((d_query, d_key, d_value, extra), axis=-1)
    packed = grads.at[slot_source].get(mode="promise_in_bounds")
    received = lax.all_to_all(packed, "enc", split_axis=0, concat_axis=0, tiled=True)
    mine = from_slots(received[:, :, : 3 * feat], arrival_order)
    parts = received[:, 0:4, 3 * feat : 3 * feat + cols].astype(jnp.float32)
    shares = jnp.sum(parts[:, 0:2] + parts[:, 2:4], axis=0)
    total_live = enc_count * grp_count * P_OWN * PIECE
    gain_grad = shares / math.sqrt(total_live)
    own_rows = P_OWN * PIECE
    mine = mine.reshape(own_rows, 3 * feat)
    return (
        mine[:, :feat],
        mine[:, feat : 2 * feat],
        mine[:, 2 * feat :],
        gain_grad,
    )


def solution(mesh):
    return jax.shard_map(
        local,
        mesh=mesh,
        in_specs=(
            P(("enc", "grp"), None),
            P(("enc", "grp"), None),
            P(("enc", "grp"), None),
            P(("enc", "grp"), None),
            P(("enc", "grp")),
            P("grp", None, None),
            P(),
        ),
        out_specs=(
            P(("enc", "grp"), None),
            P(("enc", "grp"), None),
            P(("enc", "grp"), None),
            P(None, "grp"),
        ),
        check_vma=False,
    )
```
